512 devices in a mesh: seq: 64 (over y, z), head: 8 (over x, core).
Axes of the slice: x: 4, y: 4, z: 16, core: 2. Of those that a mesh axis runs over, the one named last changes fastest.
Arguments:
- q_delta: bfloat16 [16384, 2048], P('seq', 'head'), may hold values from -6 to 6
- k_delta: bfloat16 [16384, 2048], P('seq', 'head'), may hold values from -6 to 6
- v_delta: bfloat16 [16384, 2048], P('seq', 'head'), may hold values from -6 to 6
- write_rate: float32 [16384, 16], P('seq', 'head'), may hold values from 0 to 1
- q_attn: bfloat16 [16384, 2048], P('seq', 'head'), may hold values from -200 to 200
- k_attn: bfloat16 [16384, 2048], P('seq', 'head'), may hold values from -6 to 6
- out_gain: float32 [2048], P('head'), may hold values from 0.5 to 1.5
Outputs:
- delta_out: bfloat16 [16384, 2048], P('seq', 'head')
- normed_out: bfloat16 [16384, 2048], P('seq', 'head')
The draws below stay inside these ranges and needn't reach their ends.
All inputs are finite; a program needn't handle non-finite values.
Results may differ from the reference program's by a relative error of at most 0.0058.
Values may be sent and summed in bfloat16 or wider, within the bound.
No kernel may reach another device: no remote copies, remote signals or barrier semaphores. Data moves between devices by JAX's collectives and lax.ppermute only.
A program may use at most 64 MiB of HBM per device.

```python
import math
import jax
import jax.numpy as jnp
from jax import lax

HEAD_COUNT = 16
HD = 128
GROUP_TOKENS = 64
WINDOW = 2048
TOK_DEV = 256
SEQUENCE_TOKENS = 16384
D = 2048


def draw_write_rate(key, part):
    rate_random_key, noise_random_key, block_random_key, spike_random_key = jax.random.split(jax.random.fold_in(key, 3), 4)
    slowest = 64.0 / SEQUENCE_TOKENS
    mixture = jax.random.uniform(rate_random_key, (HEAD_COUNT,))
    head_rate = jnp.exp(jnp.log(slowest) * (1.0 - mixture))
    jitter = jax.random.uniform(noise_random_key, (SEQUENCE_TOKENS, HEAD_COUNT), minval=0.5, maxval=1.5)
    block_scale = jnp.exp(jax.random.uniform(block_random_key, (SEQUENCE_TOKENS // TOK_DEV, HEAD_COUNT), minval=-0.7, maxval=0.7))
    block_scale = jnp.repeat(block_scale, TOK_DEV, axis=0)
    sampled_rate = jnp.minimum(head_rate[None, :] * jitter * block_scale, 1.0)
    spike_positions = jax.random.randint(spike_random_key, (4, HEAD_COUNT), 0, SEQUENCE_TOKENS // GROUP_TOKENS)
    group_lookup = jnp.arange(SEQUENCE_TOKENS) // GROUP_TOKENS
    inside_spike = jnp.any(group_lookup[:, None, None] == spike_positions[None, :, :], axis=1)
    return jnp.where(inside_spike, 0.9, sampled_rate).astype(jnp.float32)


def attention_pair(key):
    query_key, keys_key = jax.random.split(jax.random.fold_in(key, 7), 2)
    queries = jax.random.truncated_normal(query_key, -6.0, 6.0, (SEQUENCE_TOKENS, D), jnp.float32)
    base_keys = jax.random.truncated_normal(keys_key, -6.0, 6.0, (SEQUENCE_TOKENS, D), jnp.float32)
    key_rows = base_keys
    return (queries, key_rows)


def draw_q_attn(key, part):
    return attention_pair(key)[0].astype(jnp.bfloat16)


def draw_k_attn(key, part):
    return attention_pair(key)[1].astype(jnp.bfloat16)


def level_of(key, dims, pieces, low, high):
    factor_of = 1.0
    for dim, shards_of in pieces:
        heights = jax.random.uniform(jax.random.fold_in(jax.random.fold_in(key, 6), dim), (shards_of,), jnp.float32, low / len(pieces), high / len(pieces))
        factor_of = factor_of * jnp.repeat(jnp.exp(heights), dims[dim] // shards_of).reshape((-1,) + (1,) * (len(dims) - 1 - dim))
    return factor_of


def bell_draw(rng, shape, width, most, cuts=(), held_as=jnp.bfloat16):
    values = jax.random.normal(rng, shape, jnp.float32) * width
    if len(cuts) > 0:
        values = level_of(rng, shape, cuts, -0.22, 0.18) * values
    return jnp.clip(values, min=-most, max=most).astype(held_as)


def setup_inputs(seed: int = 0) -> dict:
    splits = jax.random.split(jax.random.key(seed), 8)
    q_delta = bell_draw(splits[0], (SEQUENCE_TOKENS, D), 1.0, 6.0, ((0, 64), (1, 8)))
    k_delta = bell_draw(splits[1], (SEQUENCE_TOKENS, D), 1.0, 6.0, ((0, 64), (1, 8)))
    v_delta = bell_draw(splits[2], (SEQUENCE_TOKENS, D), 1.0, 6.0, ((0, 64), (1, 8)))
    write_rate = draw_write_rate(jax.random.fold_in(splits[7], 71), 0)
    q_attn = draw_q_attn(jax.random.fold_in(splits[7], 71), 0)
    k_attn = draw_k_attn(jax.random.fold_in(splits[7], 71), 0)
    out_gain = jnp.clip(1.0 + 0.1 * jax.random.normal(splits[6], (D,), jnp.float32), 0.5, 1.5)
    return {"q_delta": q_delta, "k_delta": k_delta, "v_delta": v_delta, "write_rate": write_rate, "q_attn": q_attn, "k_attn": k_attn, "out_gain": out_gain}


highest = lax.Precision.HIGHEST

def unit_rows(entries):
    entries = entries.astype(jnp.float32)
    return entries * lax.rsqrt(lax.optimization_barrier(jnp.sum(entries * entries, axis=-1, keepdims=True)) + 1e-06)

def lower_inverse(below_part):
    length = below_part.shape[-1]
    identity = jnp.eye(length, dtype=jnp.float32)
    result = identity - below_part
    raised = below_part
    doubled = 2
    while doubled < length:
        raised = jnp.einsum('nij,njk->nik', raised, raised, precision=highest)
        result = jnp.einsum('nij,njk->nik', result, identity + raised, precision=highest)
        doubled = doubled * 2
    return result

def prepare(queries, key_rows, values, rate_rows):
    n_groups = queries.shape[0] // GROUP_TOKENS
    q_unit = unit_rows(queries).reshape(n_groups, GROUP_TOKENS, -1)
    k_unit = unit_rows(key_rows).reshape(n_groups, GROUP_TOKENS, -1)
    val_units = values.astype(jnp.float32).reshape(n_groups, GROUP_TOKENS, -1)
    rate_col = rate_rows.astype(jnp.float32).reshape(n_groups, GROUP_TOKENS, 1)
    key_inner = jnp.einsum('nik,njk->nij', k_unit, k_unit, precision=highest)
    positions = jnp.arange(GROUP_TOKENS)
    is_below = positions[:, None] > positions[None, :]
    on_or_below = positions[:, None] >= positions[None, :]
    below_part = jnp.where(is_below[None], rate_col * key_inner, 0.0)
    inverse = lower_inverse(below_part)
    writes = jnp.einsum('nij,njk->nik', inverse, rate_col * k_unit, precision=highest)
    updates = jnp.einsum('nij,njk->nik', inverse, rate_col * val_units, precision=highest)
    query_key = jnp.where(on_or_below[None], jnp.einsum('nik,njk->nij', q_unit, k_unit, precision=highest), 0.0)
    return (q_unit, k_unit, writes, updates, query_key)

def advance(carried, inputs_now):
    q_block, k_block, w_block, u_block, cross_block = inputs_now
    corrected = u_block - jnp.dot(w_block, carried, precision=highest)
    result_now = jnp.dot(q_block, carried, precision=highest) + jnp.dot(cross_block, corrected, precision=highest)
    return (carried + jnp.dot(k_block.T, corrected, precision=highest), result_now)

def delta_head(inputs_now):
    queries, key_rows, values, rate_rows = inputs_now
    q_unit, k_unit, writes, updates, query_key = prepare(queries, key_rows, values, rate_rows)
    head_size = queries.shape[-1]
    _, results = lax.scan(advance, jnp.zeros((head_size, head_size), jnp.float32), (q_unit, k_unit, writes, updates, query_key))
    return results.reshape(-1, head_size).astype(jnp.bfloat16)

def attend_head(inputs_now):
    queries, key_rows, values = inputs_now
    total_rows = queries.shape[0]
    head_size = queries.shape[-1]
    block_rows = min(512, total_rows)
    score_scale = 1.0 / math.sqrt(head_size)
    padding = jnp.zeros((WINDOW, head_size), jnp.float32)
    keys_padded = jnp.concatenate([padding, key_rows.astype(jnp.float32)], axis=0)
    values_padded = jnp.concatenate([padding, values.astype(jnp.float32)], axis=0)
    query_rows = queries.astype(jnp.float32)

    def attend_block(block_start):
        rows_now = lax.dynamic_slice_in_dim(query_rows, block_start, block_rows, 0)
        near_keys = lax.dynamic_slice_in_dim(keys_padded, block_start, WINDOW + block_rows, 0)
        near_values = lax.dynamic_slice_in_dim(values_padded, block_start, WINDOW + block_rows, 0)
        scores = jnp.dot(rows_now, near_keys.T) * score_scale
        q_index = jnp.arange(block_rows)[:, None]
        k_index = jnp.arange(WINDOW + block_rows)[None, :]
        allowed = (k_index > q_index) & (k_index <= q_index + WINDOW) & (block_start + k_index >= WINDOW)
        row_top = lax.optimization_barrier(jnp.max(jnp.where(allowed, scores, -1e+30), axis=1, keepdims=True))
        exps = jnp.exp(jnp.where(allowed, scores - row_top, -1e+30))
        weights = (exps / lax.optimization_barrier(jnp.sum(exps, axis=1, keepdims=True))).astype(jnp.bfloat16)
        return jnp.dot(weights.astype(jnp.float32), near_values)
    starts = (jnp.arange(total_rows // block_rows) * block_rows).astype(jnp.int32)
    return lax.map(attend_block, starts).reshape(total_rows, head_size)

def reference(q_delta, k_delta, v_delta, write_rate, q_attn, k_attn, out_gain):

    def by_head(entries):
        return entries.reshape(SEQUENCE_TOKENS, HEAD_COUNT, HD).transpose(1, 0, 2)
    delta_heads = lax.map(delta_head, (by_head(q_delta), by_head(k_delta), by_head(v_delta), write_rate.T))
    attended_heads = lax.map(attend_head, (by_head(q_attn), by_head(k_attn), delta_heads))
    delta_out = delta_heads.transpose(1, 0, 2).reshape(SEQUENCE_TOKENS, D)
    attended = attended_heads.transpose(1, 0, 2).reshape(SEQUENCE_TOKENS, D)
    width_mean = lax.optimization_barrier(jnp.mean(attended * attended, axis=1, keepdims=True))
    normed_out = (attended * out_gain[None, :] * lax.rsqrt(width_mean + 1e-06)).astype(jnp.bfloat16)
    return (delta_out, normed_out)
```

```python
import math

import jax
import jax.numpy as jnp
from jax import lax
from jax.sharding import PartitionSpec as P

GROUP_TOKENS = 64
WINDOW = 2048


highest = lax.Precision.HIGHEST


def shifted(value, axis, by):
    size = lax.axis_size(axis)
    pairs = [(i, i + by) for i in range(size) if 0 <= i + by < size]
    return lax.ppermute(value, axis, pairs)


def unit_rows(entries):
    entries = entries.astype(jnp.float32)
    return entries * lax.rsqrt(jnp.sum(entries * entries, axis=-1, keepdims=True) + 1e-06)


def lower_inverse(below_part):
    length = below_part.shape[-1]
    identity = jnp.eye(length, dtype=jnp.float32)
    result = identity - below_part
    raised = below_part
    doubled = 2
    while doubled < length:
        raised = jnp.einsum("nij,njk->nik", raised, raised, precision=highest)
        result = jnp.einsum("nij,njk->nik", result, identity + raised, precision=highest)
        doubled = doubled * 2
    return result


def prepare(queries, key_rows, values, rate_rows):
    n_groups = queries.shape[0] // GROUP_TOKENS
    q_unit = unit_rows(queries).reshape(n_groups, GROUP_TOKENS, -1)
    k_unit = unit_rows(key_rows).reshape(n_groups, GROUP_TOKENS, -1)
    val_units = values.astype(jnp.float32).reshape(n_groups, GROUP_TOKENS, -1)
    rate_col = rate_rows.reshape(n_groups, GROUP_TOKENS, 1)
    key_inner = jnp.einsum("nik,njk->nij", k_unit, k_unit, precision=highest)
    positions = jnp.arange(GROUP_TOKENS)
    is_below = positions[:, None] > positions[None, :]
    on_or_below = positions[:, None] >= positions[None, :]
    below_part = jnp.where(is_below[None], rate_col * key_inner, 0.0)
    inverse = lower_inverse(below_part)
    writes = jnp.einsum("nij,njk->nik", inverse, rate_col * k_unit, precision=highest)
    updates = jnp.einsum("nij,njk->nik", inverse, rate_col * val_units, precision=highest)
    query_key = jnp.where(
        on_or_below[None], jnp.einsum("nik,njk->nij", q_unit, k_unit, precision=highest), 0.0
    )
    return (q_unit, k_unit, writes, updates, query_key)


def local_pair(k_unit, writes, updates):
    head_size = k_unit.shape[-1]
    identity = jnp.eye(head_size, dtype=jnp.float32)

    def stride(carry, inputs_now):
        transit, carried = carry
        k_block, w_block, u_block = inputs_now
        stepped = identity - jnp.dot(k_block.T, w_block, precision=highest)
        transit = jnp.dot(stepped, transit, precision=highest)
        carried = jnp.dot(stepped, carried, precision=highest) + jnp.dot(
            k_block.T, u_block, precision=highest
        )
        return ((transit, carried), None)

    start_pair = (identity, jnp.zeros((head_size, head_size), jnp.float32))
    (transit, carried), _ = lax.scan(stride, start_pair, (k_unit, writes, updates))
    return (transit, carried)


def advance(carried, inputs_now):
    q_block, k_block, w_block, u_block, cross_block = inputs_now
    corrected = u_block - jnp.dot(w_block, carried, precision=highest)
    result_now = jnp.dot(q_block, carried, precision=highest) + jnp.dot(
        cross_block, corrected, precision=highest
    )
    return (carried + jnp.dot(k_block.T, corrected, precision=highest), result_now)


def run_blocks(carried_in, q_unit, k_unit, writes, updates, query_key):
    _, results = lax.scan(advance, carried_in, (q_unit, k_unit, writes, updates, query_key))
    return results


def batched_dot(left, right):
    return jnp.einsum("hij,hjk->hik", left, right, precision=highest)


def on_device(q_delta, k_delta, v_delta, write_rate, q_attn, k_attn, out_gain):
    tok_rows, features = q_delta.shape
    heads_here = write_rate.shape[1]
    head_size = features // heads_here

    def by_head(entries):
        return entries.reshape(tok_rows, heads_here, head_size).transpose(1, 0, 2)

    q_unit, k_unit, writes, updates, query_key = jax.vmap(prepare)(
        by_head(q_delta), by_head(k_delta), by_head(v_delta), write_rate.T
    )
    transit, carried = jax.vmap(local_pair)(k_unit, writes, updates)
    position = lax.axis_index("seq")
    seq_size = lax.axis_size("seq")
    distance = 1
    while distance < seq_size:
        final = 2 * distance >= seq_size
        if final:
            carried_prev = shifted(carried, "seq", distance)
        else:
            transit_prev, carried_prev = shifted((transit, carried), "seq", distance)
        has_prev = position >= distance
        carried = jnp.where(has_prev, batched_dot(transit, carried_prev) + carried, carried)
        if not final:
            transit = jnp.where(has_prev, batched_dot(transit, transit_prev), transit)
        distance *= 2
    incoming = shifted(carried, "seq", 1)
    results = jax.vmap(run_blocks)(incoming, q_unit, k_unit, writes, updates, query_key)
    delta_out = (
        results.reshape(heads_here, tok_rows, head_size)
        .transpose(1, 0, 2)
        .reshape(tok_rows, features)
        .astype(jnp.bfloat16)
    )
    shard_reach = WINDOW // tok_rows

    def window_rows(own):
        pieces = [own]
        for _ in range(shard_reach):
            pieces = [shifted(pieces[0], "seq", 1)] + pieces
        return jnp.concatenate(pieces, axis=0)

    rows_all = (window_rows(k_attn), window_rows(delta_out))
    block_rows = min(512, tok_rows)
    first_row = lax.axis_index("seq") * tok_rows
    score_scale = 1.0 / math.sqrt(head_size)

    def attend_block(block_start):
        queries = q_attn.reshape(block_rows, heads_here, head_size)
        near_keys = rows_all[0].reshape(WINDOW + block_rows, heads_here, head_size)
        near_values = rows_all[1].reshape(WINDOW + block_rows, heads_here, head_size)
        scores = (
            jnp.einsum("qhd,khd->hqk", queries, near_keys, preferred_element_type=jnp.float32)
            * score_scale
        )
        q_index = jnp.arange(block_rows)[:, None]
        k_index = jnp.arange(WINDOW + block_rows)[None, :]
        allowed = (
            (k_index > q_index)
            & (k_index <= q_index + WINDOW)
            & (first_row + block_start + k_index >= WINDOW)
        )
        row_top = jnp.max(jnp.where(allowed[None], scores, -1e30), axis=2, keepdims=True)
        exps = jnp.exp(jnp.where(allowed[None], scores - row_top, -1e30))
        weights = (exps / jnp.sum(exps, axis=2, keepdims=True)).astype(jnp.bfloat16)
        mixed_rows = jnp.einsum(
            "hqk,khd->qhd", weights, near_values, preferred_element_type=jnp.float32
        )
        return mixed_rows.reshape(block_rows, features)

    starts = jnp.arange(tok_rows // block_rows) * block_rows
    attended = lax.map(attend_block, starts).reshape(tok_rows, features)
    squares = jnp.sum(attended * attended, axis=1)
    total_sq = lax.psum(squares, "head")
    scale_rows = lax.rsqrt(total_sq / (features * lax.axis_size("head")) + 1e-06)
    normed_out = (attended * out_gain[None, :] * scale_rows[:, None]).astype(jnp.bfloat16)
    return (delta_out, normed_out)


def solution(mesh):
    placed = (
        P("seq", "head"),
        P("seq", "head"),
        P("seq", "head"),
        P("seq", "head"),
        P("seq", "head"),
        P("seq", "head"),
        P("head"),
    )
    return jax.shard_map(
        on_device,
        mesh=mesh,
        in_specs=placed,
        out_specs=(P("seq", "head"), P("seq", "head")),
        check_vma=False,
    )
```

```python
import math

import jax
import jax.numpy as jnp
from jax import lax
from jax.sharding import PartitionSpec as P

GROUP_TOKENS = 64
WINDOW = 2048


highest = lax.Precision.HIGHEST


def shifted(value, axis, by):
    size = lax.axis_size(axis)
    pairs = [(i, i + by) for i in range(size) if 0 <= i + by < size]
    return lax.ppermute(value, axis, pairs)


def unit_rows(entries):
    entries = entries.astype(jnp.float32)
    return entries * lax.rsqrt(jnp.sum(entries * entries, axis=-1, keepdims=True) + 1e-06)


def lower_inverse(below_part):
    length = below_part.shape[-1]
    identity = jnp.eye(length, dtype=jnp.float32)
    result = identity - below_part
    raised = below_part
    doubled = 2
    while doubled < length:
        raised = jnp.einsum("nij,njk->nik", raised, raised, precision=highest)
        result = jnp.einsum("nij,njk->nik", result, identity + raised, precision=highest)
        doubled = doubled * 2
    return result


def prepare(queries, key_rows, values, rate_rows):
    n_groups = queries.shape[0] // GROUP_TOKENS
    q_unit = unit_rows(queries).reshape(n_groups, GROUP_TOKENS, -1)
    k_unit = unit_rows(key_rows).reshape(n_groups, GROUP_TOKENS, -1)
    val_units = values.astype(jnp.float32).reshape(n_groups, GROUP_TOKENS, -1)
    rate_col = rate_rows.reshape(n_groups, GROUP_TOKENS, 1)
    key_inner = jnp.einsum("nik,njk->nij", k_unit, k_unit, precision=highest)
    positions = jnp.arange(GROUP_TOKENS)
    is_below = positions[:, None] > positions[None, :]
    on_or_below = positions[:, None] >= positions[None, :]
    below_part = jnp.where(is_below[None], rate_col * key_inner, 0.0)
    inverse = lower_inverse(below_part)
    writes = jnp.einsum("nij,njk->nik", inverse, rate_col * k_unit, precision=highest)
    updates = jnp.einsum("nij,njk->nik", inverse, rate_col * val_units, precision=highest)
    query_key = jnp.where(
        on_or_below[None], jnp.einsum("nik,njk->nij", q_unit, k_unit, precision=highest), 0.0
    )
    return (q_unit, k_unit, writes, updates, query_key)


def local_pair(k_unit, writes, updates):
    head_size = k_unit.shape[-1]
    identity = jnp.eye(head_size, dtype=jnp.float32)

    def stride(carry, inputs_now):
        transit, carried = carry
        k_block, w_block, u_block = inputs_now
        stepped = identity - jnp.dot(k_block.T, w_block, precision=highest)
        transit = jnp.dot(stepped, transit, precision=highest)
        carried = jnp.dot(stepped, carried, precision=highest) + jnp.dot(
            k_block.T, u_block, precision=highest
        )
        return ((transit, carried), None)

    start_pair = (identity, jnp.zeros((head_size, head_size), jnp.float32))
    (transit, carried), _ = lax.scan(stride, start_pair, (k_unit, writes, updates))
    return (transit, carried)


def advance(carried, inputs_now):
    q_block, k_block, w_block, u_block, cross_block = inputs_now
    corrected = u_block - jnp.dot(w_block, carried, precision=highest)
    result_now = jnp.dot(q_block, carried, precision=highest) + jnp.dot(
        cross_block, corrected, precision=highest
    )
    return (carried + jnp.dot(k_block.T, corrected, precision=highest), result_now)


def run_blocks(carried_in, q_unit, k_unit, writes, updates, query_key):
    _, results = lax.scan(advance, carried_in, (q_unit, k_unit, writes, updates, query_key))
    return results


def batched_dot(left, right):
    return jnp.einsum("hij,hjk->hik", left, right, precision=highest)


def on_device(q_delta, k_delta, v_delta, write_rate, q_attn, k_attn, out_gain):
    tok_rows, features = q_delta.shape
    heads_here = write_rate.shape[1]
    head_size = features // heads_here

    def by_head(entries):
        return entries.reshape(tok_rows, heads_here, head_size).transpose(1, 0, 2)

    q_unit, k_unit, writes, updates, query_key = jax.vmap(prepare)(
        by_head(q_delta), by_head(k_delta), by_head(v_delta), write_rate.T
    )
    transit, carried = jax.vmap(local_pair)(k_unit, writes, updates)
    position = lax.axis_index("seq")
    seq_size = lax.axis_size("seq")
    distance = 1
    while distance < seq_size:
        final = 2 * distance >= seq_size
        if final:
            carried_prev = shifted(carried, "seq", distance)
        else:
            transit_prev, carried_prev = shifted(jnp.stack((transit, carried)), "seq", distance)
        has_prev = position >= distance
        carried = jnp.where(has_prev, batched_dot(transit, carried_prev) + carried, carried)
        if not final:
            transit = jnp.where(has_prev, batched_dot(transit, transit_prev), transit)
        distance *= 2
    incoming = shifted(carried, "seq", 1)
    results = jax.vmap(run_blocks)(incoming, q_unit, k_unit, writes, updates, query_key)
    delta_out = (
        results.reshape(heads_here, tok_rows, head_size)
        .transpose(1, 0, 2)
        .reshape(tok_rows, features)
        .astype(jnp.bfloat16)
    )
    shard_reach = WINDOW // tok_rows

    def window_rows(own):
        pieces = [own]
        for _ in range(shard_reach):
            pieces = [shifted(pieces[0], "seq", 1)] + pieces
        return jnp.concatenate(pieces, axis=0)

    rows_all = (window_rows(k_attn), window_rows(delta_out))
    block_rows = min(512, tok_rows)
    first_row = lax.axis_index("seq") * tok_rows
    score_scale = 1.0 / math.sqrt(head_size)

    def attend_block(block_start):
        queries = q_attn.reshape(block_rows, heads_here, head_size)
        near_keys = rows_all[0].reshape(WINDOW + block_rows, heads_here, head_size)
        near_values = rows_all[1].reshape(WINDOW + block_rows, heads_here, head_size)
        scores = (
            jnp.einsum("qhd,khd->hqk", queries, near_keys, preferred_element_type=jnp.float32)
            * score_scale
        )
        q_index = jnp.arange(block_rows)[:, None]
        k_index = jnp.arange(WINDOW + block_rows)[None, :]
        allowed = (
            (k_index > q_index)
            & (k_index <= q_index + WINDOW)
            & (first_row + block_start + k_index >= WINDOW)
        )
        row_top = jnp.max(jnp.where(allowed[None], scores, -1e30), axis=2, keepdims=True)
        exps = jnp.exp(jnp.where(allowed[None], scores - row_top, -1e30))
        weights = (exps / jnp.sum(exps, axis=2, keepdims=True)).astype(jnp.bfloat16)
        mixed_rows = jnp.einsum(
            "hqk,khd->qhd", weights, near_values, preferred_element_type=jnp.float32
        )
        return mixed_rows.reshape(block_rows, features)

    starts = jnp.arange(tok_rows // block_rows) * block_rows
    attended = lax.map(attend_block, starts).reshape(tok_rows, features)
    squares = jnp.sum(attended * attended, axis=1)
    total_sq = squares
    head_size_axis = lax.axis_size("head")
    stride_bit = 1
    while stride_bit < head_size_axis:
        partner_pairs = [(i, i ^ stride_bit) for i in range(head_size_axis)]
        total_sq = total_sq + lax.ppermute(total_sq, "head", partner_pairs)
        stride_bit *= 2
    scale_rows = lax.rsqrt(total_sq / (features * lax.axis_size("head")) + 1e-06)
    normed_out = (attended * out_gain[None, :] * scale_rows[:, None]).astype(jnp.bfloat16)
    return (delta_out, normed_out)


def solution(mesh):
    placed = (
        P("seq", "head"),
        P("seq", "head"),
        P("seq", "head"),
        P("seq", "head"),
        P("seq", "head"),
        P("seq", "head"),
        P("head"),
    )
    return jax.shard_map(
        on_device,
        mesh=mesh,
        in_specs=placed,
        out_specs=(P("seq", "head"), P("seq", "head")),
        check_vma=False,
    )
```

```python
import math

import jax
import jax.numpy as jnp
from jax import lax
from jax.sharding import PartitionSpec as P

GROUP_TOKENS = 64
WINDOW = 2048


highest = lax.Precision.HIGHEST


def shifted(value, axis, by):
    size = lax.axis_size(axis)
    pairs = [(i, i + by) for i in range(size) if 0 <= i + by < size]
    return lax.ppermute(value, axis, pairs)


def unit_rows(entries):
    entries = entries.astype(jnp.float32)
    return entries * lax.rsqrt(jnp.sum(entries * entries, axis=-1, keepdims=True) + 1e-06)


def lower_inverse(below_part):
    length = below_part.shape[-1]
    identity = jnp.eye(length, dtype=jnp.float32)
    result = identity - below_part
    raised = below_part
    doubled = 2
    while doubled < length:
        raised = jnp.einsum("nij,njk->nik", raised, raised, precision=highest)
        result = jnp.einsum("nij,njk->nik", result, identity + raised, precision=highest)
        doubled = doubled * 2
    return result


def prepare(queries, key_rows, values, rate_rows):
    n_groups = queries.shape[0] // GROUP_TOKENS
    q_unit = unit_rows(queries).reshape(n_groups, GROUP_TOKENS, -1)
    k_unit = unit_rows(key_rows).reshape(n_groups, GROUP_TOKENS, -1)
    val_units = values.astype(jnp.float32).reshape(n_groups, GROUP_TOKENS, -1)
    rate_col = rate_rows.reshape(n_groups, GROUP_TOKENS, 1)
    key_inner = jnp.einsum("nik,njk->nij", k_unit, k_unit, precision=highest)
    positions = jnp.arange(GROUP_TOKENS)
    is_below = positions[:, None] > positions[None, :]
    on_or_below = positions[:, None] >= positions[None, :]
    below_part = jnp.where(is_below[None], rate_col * key_inner, 0.0)
    inverse = lower_inverse(below_part)
    writes = jnp.einsum("nij,njk->nik", inverse, rate_col * k_unit, precision=highest)
    updates = jnp.einsum("nij,njk->nik", inverse, rate_col * val_units, precision=highest)
    query_key = jnp.where(
        on_or_below[None], jnp.einsum("nik,njk->nij", q_unit, k_unit, precision=highest), 0.0
    )
    return (q_unit, k_unit, writes, updates, query_key)


def local_pair(k_unit, writes, updates):
    head_size = k_unit.shape[-1]
    identity = jnp.eye(head_size, dtype=jnp.float32)

    def stride(carry, inputs_now):
        transit, carried = carry
        k_block, w_block, u_block = inputs_now
        stepped = identity - jnp.dot(k_block.T, w_block, precision=highest)
        transit = jnp.dot(stepped, transit, precision=highest)
        carried = jnp.dot(stepped, carried, precision=highest) + jnp.dot(
            k_block.T, u_block, precision=highest
        )
        return ((transit, carried), None)

    start_pair = (identity, jnp.zeros((head_size, head_size), jnp.float32))
    (transit, carried), _ = lax.scan(stride, start_pair, (k_unit, writes, updates))
    return (transit, carried)


def advance(carried, inputs_now):
    q_block, k_block, w_block, u_block, cross_block = inputs_now
    corrected = u_block - jnp.dot(w_block, carried, precision=highest)
    result_now = jnp.dot(q_block, carried, precision=highest) + jnp.dot(
        cross_block, corrected, precision=highest
    )
    return (carried + jnp.dot(k_block.T, corrected, precision=highest), result_now)


def run_blocks(carried_in, q_unit, k_unit, writes, updates, query_key):
    _, results = lax.scan(advance, carried_in, (q_unit, k_unit, writes, updates, query_key))
    return results


def batched_dot(left, right):
    return jnp.einsum("hij,hjk->hik", left, right, precision=highest)


def on_device(q_delta, k_delta, v_delta, write_rate, q_attn, k_attn, out_gain):
    tok_rows, features = q_delta.shape
    heads_here = write_rate.shape[1]
    head_size = features // heads_here

    def by_head(entries):
        return entries.reshape(tok_rows, heads_here, head_size).transpose(1, 0, 2)

    q_unit, k_unit, writes, updates, query_key = jax.vmap(prepare)(
        by_head(q_delta), by_head(k_delta), by_head(v_delta), write_rate.T
    )
    transit, carried = jax.vmap(local_pair)(k_unit, writes, updates)
    position = lax.axis_index("seq")
    seq_size = lax.axis_size("seq")
    group = min(4, seq_size)
    rank = position % group

    def moved(value, by, sources):
        pairs = [(i, i + by) for i in sources if 0 <= i + by < seq_size]
        return lax.ppermute(value, "seq", pairs)

    distance = 1
    while distance < group:
        inside = [i for i in range(seq_size) if i % group + distance < group]
        transit_prev = moved(transit, distance, inside)
        carried_prev = moved(carried, distance, inside)
        has_prev = rank >= distance
        carried_in = jnp.where(has_prev, batched_dot(transit, carried_prev) + carried, carried)
        transit = jnp.where(has_prev, batched_dot(transit, transit_prev), transit)
        carried = carried_in
        distance *= 2
    ends = [i for i in range(seq_size) if i % group == group - 1]
    end_transit, end_carried = transit, carried
    distance = group
    while distance < seq_size:
        final = 2 * distance >= seq_size
        carried_prev = moved(end_carried, distance, ends)
        has_prev = (rank == group - 1) & (position >= distance)
        carried_next = jnp.where(
            has_prev, batched_dot(end_transit, carried_prev) + end_carried, end_carried
        )
        if not final:
            transit_prev = moved(end_transit, distance, ends)
            end_transit = jnp.where(has_prev, batched_dot(end_transit, transit_prev), end_transit)
        end_carried = carried_next
        distance *= 2
    group_in = jnp.zeros_like(carried)
    for hop in range(1, group):
        group_in = group_in + moved(end_carried, hop, ends)
    leaving = jnp.where(
        rank == group - 1, end_carried, batched_dot(transit, group_in) + carried
    )
    incoming = shifted(leaving, "seq", 1)
    results = jax.vmap(run_blocks)(incoming, q_unit, k_unit, writes, updates, query_key)
    delta_out = (
        results.reshape(heads_here, tok_rows, head_size)
        .transpose(1, 0, 2)
        .reshape(tok_rows, features)
        .astype(jnp.bfloat16)
    )
    shard_reach = WINDOW // tok_rows

    def window_rows(own):
        pieces = [own]
        for _ in range(shard_reach):
            pieces = [shifted(pieces[0], "seq", 1)] + pieces
        return jnp.concatenate(pieces, axis=0)

    rows_all = (window_rows(k_attn), window_rows(delta_out))
    block_rows = min(512, tok_rows)
    first_row = lax.axis_index("seq") * tok_rows
    score_scale = 1.0 / math.sqrt(head_size)

    def attend_block(block_start):
        queries = q_attn.reshape(block_rows, heads_here, head_size)
        near_keys = rows_all[0].reshape(WINDOW + block_rows, heads_here, head_size)
        near_values = rows_all[1].reshape(WINDOW + block_rows, heads_here, head_size)
        scores = (
            jnp.einsum("qhd,khd->hqk", queries, near_keys, preferred_element_type=jnp.float32)
            * score_scale
        )
        q_index = jnp.arange(block_rows)[:, None]
        k_index = jnp.arange(WINDOW + block_rows)[None, :]
        allowed = (
            (k_index > q_index)
            & (k_index <= q_index + WINDOW)
            & (first_row + block_start + k_index >= WINDOW)
        )
        row_top = jnp.max(jnp.where(allowed[None], scores, -1e30), axis=2, keepdims=True)
        exps = jnp.exp(jnp.where(allowed[None], scores - row_top, -1e30))
        weights = (exps / jnp.sum(exps, axis=2, keepdims=True)).astype(jnp.bfloat16)
        mixed_rows = jnp.einsum(
            "hqk,khd->qhd", weights, near_values, preferred_element_type=jnp.float32
        )
        return mixed_rows.reshape(block_rows, features)

    starts = jnp.arange(tok_rows // block_rows) * block_rows
    attended = lax.map(attend_block, starts).reshape(tok_rows, features)
    squares = jnp.sum(attended * attended, axis=1)
    total_sq = lax.psum(squares, "head")
    scale_rows = lax.rsqrt(total_sq / (features * lax.axis_size("head")) + 1e-06)
    normed_out = (attended * out_gain[None, :] * scale_rows[:, None]).astype(jnp.bfloat16)
    return (delta_out, normed_out)


def solution(mesh):
    placed = (
        P("seq", "head"),
        P("seq", "head"),
        P("seq", "head"),
        P("seq", "head"),
        P("seq", "head"),
        P("seq", "head"),
        P("head"),
    )
    return jax.shard_map(
        on_device,
        mesh=mesh,
        in_specs=placed,
        out_specs=(P("seq", "head"), P("seq", "head")),
        check_vma=False,
    )
```

```python
import math

import jax
import jax.numpy as jnp
from jax import lax
from jax.sharding import PartitionSpec as P

GROUP_TOKENS = 64
WINDOW = 2048


highest = lax.Precision.HIGHEST


def shifted(value, axis, by):
    size = lax.axis_size(axis)
    pairs = [(i, i + by) for i in range(size) if 0 <= i + by < size]
    return lax.ppermute(value, axis, pairs)


def unit_rows(entries):
    entries = entries.astype(jnp.float32)
    return entries * lax.rsqrt(jnp.sum(entries * entries, axis=-1, keepdims=True) + 1e-06)


def lower_inverse(below_part):
    length = below_part.shape[-1]
    identity = jnp.eye(length, dtype=jnp.float32)
    result = identity - below_part
    raised = below_part
    doubled = 2
    while doubled < length:
        raised = jnp.einsum("nij,njk->nik", raised, raised, precision=highest)
        result = jnp.einsum("nij,njk->nik", result, identity + raised, precision=highest)
        doubled = doubled * 2
    return result


def prepare(queries, key_rows, values, rate_rows):
    n_groups = queries.shape[0] // GROUP_TOKENS
    q_unit = unit_rows(queries).reshape(n_groups, GROUP_TOKENS, -1)
    k_unit = unit_rows(key_rows).reshape(n_groups, GROUP_TOKENS, -1)
    val_units = values.astype(jnp.float32).reshape(n_groups, GROUP_TOKENS, -1)
    rate_col = rate_rows.reshape(n_groups, GROUP_TOKENS, 1)
    key_inner = jnp.einsum("nik,njk->nij", k_unit, k_unit, precision=highest)
    positions = jnp.arange(GROUP_TOKENS)
    is_below = positions[:, None] > positions[None, :]
    on_or_below = positions[:, None] >= positions[None, :]
    below_part = jnp.where(is_below[None], rate_col * key_inner, 0.0)
    inverse = lower_inverse(below_part)
    writes = jnp.einsum("nij,njk->nik", inverse, rate_col * k_unit, precision=highest)
    updates = jnp.einsum("nij,njk->nik", inverse, rate_col * val_units, precision=highest)
    query_key = jnp.where(
        on_or_below[None], jnp.einsum("nik,njk->nij", q_unit, k_unit, precision=highest), 0.0
    )
    return (q_unit, k_unit, writes, updates, query_key)


def local_pair(k_unit, writes, updates):
    head_size = k_unit.shape[-1]
    identity = jnp.eye(head_size, dtype=jnp.float32)

    def stride(carry, inputs_now):
        transit, carried = carry
        k_block, w_block, u_block = inputs_now
        stepped = identity - jnp.dot(k_block.T, w_block, precision=highest)
        transit = jnp.dot(stepped, transit, precision=highest)
        carried = jnp.dot(stepped, carried, precision=highest) + jnp.dot(
            k_block.T, u_block, precision=highest
        )
        return ((transit, carried), None)

    start_pair = (identity, jnp.zeros((head_size, head_size), jnp.float32))
    (transit, carried), _ = lax.scan(stride, start_pair, (k_unit, writes, updates))
    return (transit, carried)


def advance(carried, inputs_now):
    q_block, k_block, w_block, u_block, cross_block = inputs_now
    corrected = u_block - jnp.dot(w_block, carried, precision=highest)
    result_now = jnp.dot(q_block, carried, precision=highest) + jnp.dot(
        cross_block, corrected, precision=highest
    )
    return (carried + jnp.dot(k_block.T, corrected, precision=highest), result_now)


def run_blocks(carried_in, q_unit, k_unit, writes, updates, query_key):
    _, results = lax.scan(advance, carried_in, (q_unit, k_unit, writes, updates, query_key))
    return results


def batched_dot(left, right):
    return jnp.einsum("hij,hjk->hik", left, right, precision=highest)


def on_device(q_delta, k_delta, v_delta, write_rate, q_attn, k_attn, out_gain):
    tok_rows, features = q_delta.shape
    heads_here = write_rate.shape[1]
    head_size = features // heads_here

    def by_head(entries):
        return entries.reshape(tok_rows, heads_here, head_size).transpose(1, 0, 2)

    q_unit, k_unit, writes, updates, query_key = jax.vmap(prepare)(
        by_head(q_delta), by_head(k_delta), by_head(v_delta), write_rate.T
    )
    transit, carried = jax.vmap(local_pair)(k_unit, writes, updates)
    position = lax.axis_index("seq")
    seq_size = lax.axis_size("seq")
    group = min(4, seq_size)
    rank = position % group

    def moved(value, by, sources):
        pairs = [(i, i + by) for i in sources if 0 <= i + by < seq_size]
        return lax.ppermute(value, "seq", pairs)

    distance = 1
    while distance < group:
        inside = [i for i in range(seq_size) if i % group + distance < group]
        transit_prev = moved(transit, distance, inside)
        carried_prev = moved(carried, distance, inside)
        has_prev = rank >= distance
        carried_in = jnp.where(has_prev, batched_dot(transit, carried_prev) + carried, carried)
        transit = jnp.where(has_prev, batched_dot(transit, transit_prev), transit)
        carried = carried_in
        distance *= 2
    ends = [i for i in range(seq_size) if i % group == group - 1]
    end_transit, end_carried = transit, carried
    distance = group
    while distance < seq_size:
        final = 2 * distance >= seq_size
        carried_prev = moved(end_carried, distance, ends)
        has_prev = (rank == group - 1) & (position >= distance)
        carried_next = jnp.where(
            has_prev, batched_dot(end_transit, carried_prev) + end_carried, end_carried
        )
        if not final:
            transit_prev = moved(end_transit, distance, ends)
            end_transit = jnp.where(has_prev, batched_dot(end_transit, transit_prev), end_transit)
        end_carried = carried_next
        distance *= 2
    group_in = jnp.zeros_like(carried)
    for hop in range(1, group):
        group_in = group_in + moved(end_carried, hop, ends)
    leaving = jnp.where(
        rank == group - 1, end_carried, batched_dot(transit, group_in) + carried
    )
    incoming = shifted(leaving, "seq", 1)
    results = jax.vmap(run_blocks)(incoming, q_unit, k_unit, writes, updates, query_key)
    delta_out = (
        results.reshape(heads_here, tok_rows, head_size)
        .transpose(1, 0, 2)
        .reshape(tok_rows, features)
        .astype(jnp.bfloat16)
    )
    shard_reach = WINDOW // tok_rows

    def window_rows(own):
        pieces = [own]
        for _ in range(shard_reach):
            pieces = [shifted(pieces[0], "seq", 1)] + pieces
        return jnp.concatenate(pieces, axis=0)

    rows_all = window_rows(jnp.stack((k_attn, delta_out), axis=1))
    rows_all = (rows_all[:, 0], rows_all[:, 1])
    block_rows = min(512, tok_rows)
    first_row = lax.axis_index("seq") * tok_rows
    score_scale = 1.0 / math.sqrt(head_size)

    def attend_block(block_start):
        queries = q_attn.reshape(block_rows, heads_here, head_size)
        near_keys = rows_all[0].reshape(WINDOW + block_rows, heads_here, head_size)
        near_values = rows_all[1].reshape(WINDOW + block_rows, heads_here, head_size)
        scores = (
            jnp.einsum("qhd,khd->hqk", queries, near_keys, preferred_element_type=jnp.float32)
            * score_scale
        )
        q_index = jnp.arange(block_rows)[:, None]
        k_index = jnp.arange(WINDOW + block_rows)[None, :]
        allowed = (
            (k_index > q_index)
            & (k_index <= q_index + WINDOW)
            & (first_row + block_start + k_index >= WINDOW)
        )
        row_top = jnp.max(jnp.where(allowed[None], scores, -1e30), axis=2, keepdims=True)
        exps = jnp.exp(jnp.where(allowed[None], scores - row_top, -1e30))
        weights = (exps / jnp.sum(exps, axis=2, keepdims=True)).astype(jnp.bfloat16)
        mixed_rows = jnp.einsum(
            "hqk,khd->qhd", weights, near_values, preferred_element_type=jnp.float32
        )
        return mixed_rows.reshape(block_rows, features)

    starts = jnp.arange(tok_rows // block_rows) * block_rows
    attended = lax.map(attend_block, starts).reshape(tok_rows, features)
    squares = jnp.sum(attended * attended, axis=1)
    total_sq = lax.psum(squares, "head")
    scale_rows = lax.rsqrt(total_sq / (features * lax.axis_size("head")) + 1e-06)
    normed_out = (attended * out_gain[None, :] * scale_rows[:, None]).astype(jnp.bfloat16)
    return (delta_out, normed_out)


def solution(mesh):
    placed = (
        P("seq", "head"),
        P("seq", "head"),
        P("seq", "head"),
        P("seq", "head"),
        P("seq", "head"),
        P("seq", "head"),
        P("head"),
    )
    return jax.shard_map(
        on_device,
        mesh=mesh,
        in_specs=placed,
        out_specs=(P("seq", "head"), P("seq", "head")),
        check_vma=False,
    )
```

```python
import math

import jax
import jax.numpy as jnp
from jax import lax
from jax.sharding import PartitionSpec as P

GROUP_TOKENS = 64
WINDOW = 2048


highest = lax.Precision.HIGHEST


def shifted(value, axis, by):
    size = lax.axis_size(axis)
    pairs = [(i, i + by) for i in range(size) if 0 <= i + by < size]
    return lax.ppermute(value, axis, pairs)


def unit_rows(entries):
    entries = entries.astype(jnp.float32)
    return entries * lax.rsqrt(jnp.sum(entries * entries, axis=-1, keepdims=True) + 1e-06)


def lower_inverse(below_part):
    length = below_part.shape[-1]
    identity = jnp.eye(length, dtype=jnp.float32)
    result = identity - below_part
    raised = below_part
    doubled = 2
    while doubled < length:
        raised = jnp.einsum("nij,njk->nik", raised, raised, precision=highest)
        result = jnp.einsum("nij,njk->nik", result, identity + raised, precision=highest)
        doubled = doubled * 2
    return result


def prepare(queries, key_rows, values, rate_rows):
    n_groups = queries.shape[0] // GROUP_TOKENS
    q_unit = unit_rows(queries).reshape(n_groups, GROUP_TOKENS, -1)
    k_unit = unit_rows(key_rows).reshape(n_groups, GROUP_TOKENS, -1)
    val_units = values.astype(jnp.float32).reshape(n_groups, GROUP_TOKENS, -1)
    rate_col = rate_rows.reshape(n_groups, GROUP_TOKENS, 1)
    key_inner = jnp.einsum("nik,njk->nij", k_unit, k_unit, precision=highest)
    positions = jnp.arange(GROUP_TOKENS)
    is_below = positions[:, None] > positions[None, :]
    on_or_below = positions[:, None] >= positions[None, :]
    below_part = jnp.where(is_below[None], rate_col * key_inner, 0.0)
    inverse = lower_inverse(below_part)
    writes = jnp.einsum("nij,njk->nik", inverse, rate_col * k_unit, precision=highest)
    updates = jnp.einsum("nij,njk->nik", inverse, rate_col * val_units, precision=highest)
    query_key = jnp.where(
        on_or_below[None], jnp.einsum("nik,njk->nij", q_unit, k_unit, precision=highest), 0.0
    )
    return (q_unit, k_unit, writes, updates, query_key)


def local_pair(k_unit, writes, updates):
    head_size = k_unit.shape[-1]
    identity = jnp.eye(head_size, dtype=jnp.float32)

    def stride(carry, inputs_now):
        transit, carried = carry
        k_block, w_block, u_block = inputs_now
        stepped = identity - jnp.dot(k_block.T, w_block, precision=highest)
        transit = jnp.dot(stepped, transit, precision=highest)
        carried = jnp.dot(stepped, carried, precision=highest) + jnp.dot(
            k_block.T, u_block, precision=highest
        )
        return ((transit, carried), None)

    start_pair = (identity, jnp.zeros((head_size, head_size), jnp.float32))
    (transit, carried), _ = lax.scan(stride, start_pair, (k_unit, writes, updates))
    return (transit, carried)


def advance(carried, inputs_now):
    q_block, k_block, w_block, u_block, cross_block = inputs_now
    corrected = u_block - jnp.dot(w_block, carried, precision=highest)
    result_now = jnp.dot(q_block, carried, precision=highest) + jnp.dot(
        cross_block, corrected, precision=highest
    )
    return (carried + jnp.dot(k_block.T, corrected, precision=highest), result_now)


def run_blocks(carried_in, q_unit, k_unit, writes, updates, query_key):
    _, results = lax.scan(advance, carried_in, (q_unit, k_unit, writes, updates, query_key))
    return results


def batched_dot(left, right):
    return jnp.einsum("hij,hjk->hik", left, right, precision=highest)


def on_device(q_delta, k_delta, v_delta, write_rate, q_attn, k_attn, out_gain):
    tok_rows, features = q_delta.shape
    heads_here = write_rate.shape[1]
    head_size = features // heads_here

    def by_head(entries):
        return entries.reshape(tok_rows, heads_here, head_size).transpose(1, 0, 2)

    q_unit, k_unit, writes, updates, query_key = jax.vmap(prepare)(
        by_head(q_delta), by_head(k_delta), by_head(v_delta), write_rate.T
    )
    transit, carried = jax.vmap(local_pair)(k_unit, writes, updates)
    position = lax.axis_index("seq")
    seq_size = lax.axis_size("seq")
    group = min(4, seq_size)
    rank = position % group

    def moved(value, by, sources):
        pairs = [(i, i + by) for i in sources if 0 <= i + by < seq_size]
        return lax.ppermute(value, "seq", pairs)

    identity = jnp.broadcast_to(jnp.eye(head_size, dtype=jnp.float32), transit.shape)
    before_transit = identity
    before_carried = jnp.zeros_like(carried)
    distance = 1
    while distance < group:
        inside = [i for i in range(seq_size) if i % group + distance < group]
        transit_prev = moved(transit, distance, inside)
        carried_prev = moved(carried, distance, inside)
        has_prev = rank >= distance
        before_carried = jnp.where(
            has_prev, batched_dot(before_transit, carried_prev) + before_carried, before_carried
        )
        before_transit = jnp.where(has_prev, batched_dot(before_transit, transit_prev), before_transit)
        carried_in = jnp.where(has_prev, batched_dot(transit, carried_prev) + carried, carried)
        transit = jnp.where(has_prev, batched_dot(transit, transit_prev), transit)
        carried = carried_in
        distance *= 2
    ends = [i for i in range(seq_size) if i % group == group - 1]
    end_transit, end_carried = transit, carried
    distance = group
    while distance < seq_size:
        final = 2 * distance >= seq_size
        carried_prev = moved(end_carried, distance, ends)
        has_prev = (rank == group - 1) & (position >= distance)
        carried_next = jnp.where(
            has_prev, batched_dot(end_transit, carried_prev) + end_carried, end_carried
        )
        if not final:
            transit_prev = moved(end_transit, distance, ends)
            end_transit = jnp.where(has_prev, batched_dot(end_transit, transit_prev), end_transit)
        end_carried = carried_next
        distance *= 2
    group_in = jnp.zeros_like(carried)
    for hop in range(1, group + 1):
        group_in = group_in + moved(end_carried, hop, ends)
    incoming = batched_dot(before_transit, group_in) + before_carried
    results = jax.vmap(run_blocks)(incoming, q_unit, k_unit, writes, updates, query_key)
    delta_out = (
        results.reshape(heads_here, tok_rows, head_size)
        .transpose(1, 0, 2)
        .reshape(tok_rows, features)
        .astype(jnp.bfloat16)
    )
    shard_reach = WINDOW // tok_rows

    def window_rows(own):
        pieces = [own]
        for _ in range(shard_reach):
            pieces = [shifted(pieces[0], "seq", 1)] + pieces
        return jnp.concatenate(pieces, axis=0)

    rows_all = (window_rows(k_attn), window_rows(delta_out))
    block_rows = min(512, tok_rows)
    first_row = lax.axis_index("seq") * tok_rows
    score_scale = 1.0 / math.sqrt(head_size)

    def attend_block(block_start):
        queries = q_attn.reshape(block_rows, heads_here, head_size)
        near_keys = rows_all[0].reshape(WINDOW + block_rows, heads_here, head_size)
        near_values = rows_all[1].reshape(WINDOW + block_rows, heads_here, head_size)
        scores = (
            jnp.einsum("qhd,khd->hqk", queries, near_keys, preferred_element_type=jnp.float32)
            * score_scale
        )
        q_index = jnp.arange(block_rows)[:, None]
        k_index = jnp.arange(WINDOW + block_rows)[None, :]
        allowed = (
            (k_index > q_index)
            & (k_index <= q_index + WINDOW)
            & (first_row + block_start + k_index >= WINDOW)
        )
        row_top = jnp.max(jnp.where(allowed[None], scores, -1e30), axis=2, keepdims=True)
        exps = jnp.exp(jnp.where(allowed[None], scores - row_top, -1e30))
        weights = (exps / jnp.sum(exps, axis=2, keepdims=True)).astype(jnp.bfloat16)
        mixed_rows = jnp.einsum(
            "hqk,khd->qhd", weights, near_values, preferred_element_type=jnp.float32
        )
        return mixed_rows.reshape(block_rows, features)

    starts = jnp.arange(tok_rows // block_rows) * block_rows
    attended = lax.map(attend_block, starts).reshape(tok_rows, features)
    squares = jnp.sum(attended * attended, axis=1)
    total_sq = lax.psum(squares, "head")
    scale_rows = lax.rsqrt(total_sq / (features * lax.axis_size("head")) + 1e-06)
    normed_out = (attended * out_gain[None, :] * scale_rows[:, None]).astype(jnp.bfloat16)
    return (delta_out, normed_out)


def solution(mesh):
    placed = (
        P("seq", "head"),
        P("seq", "head"),
        P("seq", "head"),
        P("seq", "head"),
        P("seq", "head"),
        P("seq", "head"),
        P("head"),
    )
    return jax.shard_map(
        on_device,
        mesh=mesh,
        in_specs=placed,
        out_specs=(P("seq", "head"), P("seq", "head")),
        check_vma=False,
    )
```

```python
import math

import jax
import jax.numpy as jnp
from jax import lax
from jax.sharding import PartitionSpec as P

GROUP_TOKENS = 64
WINDOW = 2048


highest = lax.Precision.HIGHEST


def shifted(value, axis, by):
    size = lax.axis_size(axis)
    pairs = [(i, i + by) for i in range(size) if 0 <= i + by < size]
    return lax.ppermute(value, axis, pairs)


def unit_rows(entries):
    entries = entries.astype(jnp.float32)
    return entries * lax.rsqrt(jnp.sum(entries * entries, axis=-1, keepdims=True) + 1e-06)


def lower_inverse(below_part):
    length = below_part.shape[-1]
    identity = jnp.eye(length, dtype=jnp.float32)
    result = identity - below_part
    raised = below_part
    doubled = 2
    while doubled < length:
        raised = jnp.einsum("nij,njk->nik", raised, raised, precision=highest)
        result = jnp.einsum("nij,njk->nik", result, identity + raised, precision=highest)
        doubled = doubled * 2
    return result


def prepare(queries, key_rows, values, rate_rows):
    n_groups = queries.shape[0] // GROUP_TOKENS
    q_unit = unit_rows(queries).reshape(n_groups, GROUP_TOKENS, -1)
    k_unit = unit_rows(key_rows).reshape(n_groups, GROUP_TOKENS, -1)
    val_units = values.astype(jnp.float32).reshape(n_groups, GROUP_TOKENS, -1)
    rate_col = rate_rows.reshape(n_groups, GROUP_TOKENS, 1)
    key_inner = jnp.einsum("nik,njk->nij", k_unit, k_unit, precision=highest)
    positions = jnp.arange(GROUP_TOKENS)
    is_below = positions[:, None] > positions[None, :]
    on_or_below = positions[:, None] >= positions[None, :]
    below_part = jnp.where(is_below[None], rate_col * key_inner, 0.0)
    inverse = lower_inverse(below_part)
    writes = jnp.einsum("nij,njk->nik", inverse, rate_col * k_unit, precision=highest)
    updates = jnp.einsum("nij,njk->nik", inverse, rate_col * val_units, precision=highest)
    query_key = jnp.where(
        on_or_below[None], jnp.einsum("nik,njk->nij", q_unit, k_unit, precision=highest), 0.0
    )
    return (q_unit, k_unit, writes, updates, query_key)


def local_pair(k_unit, writes, updates):
    head_size = k_unit.shape[-1]
    identity = jnp.eye(head_size, dtype=jnp.float32)

    def stride(carry, inputs_now):
        transit, carried = carry
        k_block, w_block, u_block = inputs_now
        stepped = identity - jnp.dot(k_block.T, w_block, precision=highest)
        transit = jnp.dot(stepped, transit, precision=highest)
        carried = jnp.dot(stepped, carried, precision=highest) + jnp.dot(
            k_block.T, u_block, precision=highest
        )
        return ((transit, carried), None)

    start_pair = (identity, jnp.zeros((head_size, head_size), jnp.float32))
    (transit, carried), _ = lax.scan(stride, start_pair, (k_unit, writes, updates))
    return (transit, carried)


def advance(carried, inputs_now):
    q_block, k_block, w_block, u_block, cross_block = inputs_now
    corrected = u_block - jnp.dot(w_block, carried, precision=highest)
    result_now = jnp.dot(q_block, carried, precision=highest) + jnp.dot(
        cross_block, corrected, precision=highest
    )
    return (carried + jnp.dot(k_block.T, corrected, precision=highest), result_now)


def run_blocks(carried_in, q_unit, k_unit, writes, updates, query_key):
    _, results = lax.scan(advance, carried_in, (q_unit, k_unit, writes, updates, query_key))
    return results


def batched_dot(left, right):
    return jnp.einsum("hij,hjk->hik", left, right, precision=highest)


def on_device(q_delta, k_delta, v_delta, write_rate, q_attn, k_attn, out_gain):
    tok_rows, features = q_delta.shape
    heads_here = write_rate.shape[1]
    head_size = features // heads_here

    def by_head(entries):
        return entries.reshape(tok_rows, heads_here, head_size).transpose(1, 0, 2)

    q_unit, k_unit, writes, updates, query_key = jax.vmap(prepare)(
        by_head(q_delta), by_head(k_delta), by_head(v_delta), write_rate.T
    )
    transit, carried = jax.vmap(local_pair)(k_unit, writes, updates)
    position = lax.axis_index("seq")
    seq_size = lax.axis_size("seq")
    group = min(4, seq_size)
    rank = position % group

    def moved(value, by, sources):
        pairs = [(i, i + by) for i in sources if 0 <= i + by < seq_size]
        return lax.ppermute(value, "seq", pairs)

    identity = jnp.broadcast_to(jnp.eye(head_size, dtype=jnp.float32), transit.shape)
    before_transit = identity
    before_carried = jnp.zeros_like(carried)
    distance = 1
    while distance < group:
        inside = [i for i in range(seq_size) if i % group + distance < group]
        transit_prev = moved(transit, distance, inside)
        carried_prev = moved(carried, distance, inside)
        has_prev = rank >= distance
        before_carried = jnp.where(
            has_prev, batched_dot(before_transit, carried_prev) + before_carried, before_carried
        )
        before_transit = jnp.where(has_prev, batched_dot(before_transit, transit_prev), before_transit)
        carried_in = jnp.where(has_prev, batched_dot(transit, carried_prev) + carried, carried)
        transit = jnp.where(has_prev, batched_dot(transit, transit_prev), transit)
        carried = carried_in
        distance *= 2
    ends = [i for i in range(seq_size) if i % group == group - 1]
    end_transit, end_carried = transit, carried
    distance = group
    while distance < seq_size:
        final = 2 * distance >= seq_size
        carried_prev = moved(end_carried, distance, ends)
        has_prev = (rank == group - 1) & (position >= distance)
        carried_next = jnp.where(
            has_prev, batched_dot(end_transit, carried_prev) + end_carried, end_carried
        )
        if not final:
            transit_prev = moved(end_transit, distance, ends)
            end_transit = jnp.where(has_prev, batched_dot(end_transit, transit_prev), end_transit)
        end_carried = carried_next
        distance *= 2
    group_in = jnp.zeros_like(carried)
    for hop in range(1, group + 1):
        group_in = group_in + moved(end_carried, hop, ends)
    incoming = batched_dot(before_transit, group_in) + before_carried
    results = jax.vmap(run_blocks)(incoming, q_unit, k_unit, writes, updates, query_key)
    delta_out = (
        results.reshape(heads_here, tok_rows, head_size)
        .transpose(1, 0, 2)
        .reshape(tok_rows, features)
        .astype(jnp.bfloat16)
    )
    shard_reach = WINDOW // tok_rows

    def window_rows(own, lanes):
        lane_length = -(-shard_reach // lanes)
        pieces = []
        for lane in range(lanes):
            first = lane * lane_length + 1
            last = min(shard_reach, (lane + 1) * lane_length)
            piece = shifted(own, "seq", first)
            pieces.append(piece)
            for _ in range(first, last):
                piece = shifted(piece, "seq", 1)
                pieces.append(piece)
        return jnp.concatenate(pieces[::-1] + [own], axis=0)

    rows_all = (window_rows(k_attn, 1), window_rows(delta_out, 2))
    block_rows = min(512, tok_rows)
    first_row = lax.axis_index("seq") * tok_rows
    score_scale = 1.0 / math.sqrt(head_size)

    def attend_block(block_start):
        queries = q_attn.reshape(block_rows, heads_here, head_size)
        near_keys = rows_all[0].reshape(WINDOW + block_rows, heads_here, head_size)
        near_values = rows_all[1].reshape(WINDOW + block_rows, heads_here, head_size)
        scores = (
            jnp.einsum("qhd,khd->hqk", queries, near_keys, preferred_element_type=jnp.float32)
            * score_scale
        )
        q_index = jnp.arange(block_rows)[:, None]
        k_index = jnp.arange(WINDOW + block_rows)[None, :]
        allowed = (
            (k_index > q_index)
            & (k_index <= q_index + WINDOW)
            & (first_row + block_start + k_index >= WINDOW)
        )
        row_top = jnp.max(jnp.where(allowed[None], scores, -1e30), axis=2, keepdims=True)
        exps = jnp.exp(jnp.where(allowed[None], scores - row_top, -1e30))
        weights = (exps / jnp.sum(exps, axis=2, keepdims=True)).astype(jnp.bfloat16)
        mixed_rows = jnp.einsum(
            "hqk,khd->qhd", weights, near_values, preferred_element_type=jnp.float32
        )
        return mixed_rows.reshape(block_rows, features)

    starts = jnp.arange(tok_rows // block_rows) * block_rows
    attended = lax.map(attend_block, starts).reshape(tok_rows, features)
    squares = jnp.sum(attended * attended, axis=1)
    total_sq = lax.psum(squares, "head")
    scale_rows = lax.rsqrt(total_sq / (features * lax.axis_size("head")) + 1e-06)
    normed_out = (attended * out_gain[None, :] * scale_rows[:, None]).astype(jnp.bfloat16)
    return (delta_out, normed_out)


def solution(mesh):
    placed = (
        P("seq", "head"),
        P("seq", "head"),
        P("seq", "head"),
        P("seq", "head"),
        P("seq", "head"),
        P("seq", "head"),
        P("head"),
    )
    return jax.shard_map(
        on_device,
        mesh=mesh,
        in_specs=placed,
        out_specs=(P("seq", "head"), P("seq", "head")),
        check_vma=False,
    )
```

```python
import math

import jax
import jax.numpy as jnp
from jax import lax
from jax.sharding import PartitionSpec as P

GROUP_TOKENS = 64
WINDOW = 2048


highest = lax.Precision.HIGHEST


def shifted(value, axis, by):
    size = lax.axis_size(axis)
    pairs = [(i, i + by) for i in range(size) if 0 <= i + by < size]
    return lax.ppermute(value, axis, pairs)


def unit_rows(entries):
    entries = entries.astype(jnp.float32)
    return entries * lax.rsqrt(jnp.sum(entries * entries, axis=-1, keepdims=True) + 1e-06)


def lower_inverse(below_part):
    length = below_part.shape[-1]
    identity = jnp.eye(length, dtype=jnp.float32)
    result = identity - below_part
    raised = below_part
    doubled = 2
    while doubled < length:
        raised = jnp.einsum("nij,njk->nik", raised, raised, precision=highest)
        result = jnp.einsum("nij,njk->nik", result, identity + raised, precision=highest)
        doubled = doubled * 2
    return result


def prepare(queries, key_rows, values, rate_rows):
    n_groups = queries.shape[0] // GROUP_TOKENS
    q_unit = unit_rows(queries).reshape(n_groups, GROUP_TOKENS, -1)
    k_unit = unit_rows(key_rows).reshape(n_groups, GROUP_TOKENS, -1)
    val_units = values.astype(jnp.float32).reshape(n_groups, GROUP_TOKENS, -1)
    rate_col = rate_rows.reshape(n_groups, GROUP_TOKENS, 1)
    key_inner = jnp.einsum("nik,njk->nij", k_unit, k_unit, precision=highest)
    positions = jnp.arange(GROUP_TOKENS)
    is_below = positions[:, None] > positions[None, :]
    on_or_below = positions[:, None] >= positions[None, :]
    below_part = jnp.where(is_below[None], rate_col * key_inner, 0.0)
    inverse = lower_inverse(below_part)
    writes = jnp.einsum("nij,njk->nik", inverse, rate_col * k_unit, precision=highest)
    updates = jnp.einsum("nij,njk->nik", inverse, rate_col * val_units, precision=highest)
    query_key = jnp.where(
        on_or_below[None], jnp.einsum("nik,njk->nij", q_unit, k_unit, precision=highest), 0.0
    )
    return (q_unit, k_unit, writes, updates, query_key)


def local_pair(k_unit, writes, updates):
    head_size = k_unit.shape[-1]
    identity = jnp.eye(head_size, dtype=jnp.float32)
    key_cols = jnp.swapaxes(k_unit, -1, -2)
    transit = identity - jnp.einsum("nij,njk->nik", key_cols, writes, precision=highest)
    carried = jnp.einsum("nij,njk->nik", key_cols, updates, precision=highest)
    while transit.shape[0] > 1:
        if transit.shape[0] % 2:
            transit = jnp.concatenate([identity[None], transit], axis=0)
            carried = jnp.concatenate([jnp.zeros_like(carried[:1]), carried], axis=0)
        early_t, late_t = transit[0::2], transit[1::2]
        early_c, late_c = carried[0::2], carried[1::2]
        transit = jnp.einsum("nij,njk->nik", late_t, early_t, precision=highest)
        carried = jnp.einsum("nij,njk->nik", late_t, early_c, precision=highest) + late_c
    return (transit[0], carried[0])


def advance(carried, inputs_now):
    q_block, k_block, w_block, u_block, cross_block = inputs_now
    corrected = u_block - jnp.dot(w_block, carried, precision=highest)
    result_now = jnp.dot(q_block, carried, precision=highest) + jnp.dot(
        cross_block, corrected, precision=highest
    )
    return (carried + jnp.dot(k_block.T, corrected, precision=highest), result_now)


def run_blocks(carried_in, q_unit, k_unit, writes, updates, query_key):
    _, results = lax.scan(advance, carried_in, (q_unit, k_unit, writes, updates, query_key))
    return results


def batched_dot(left, right):
    return jnp.einsum("hij,hjk->hik", left, right, precision=highest)


def on_device(q_delta, k_delta, v_delta, write_rate, q_attn, k_attn, out_gain):
    tok_rows, features = q_delta.shape
    heads_here = write_rate.shape[1]
    head_size = features // heads_here

    def by_head(entries):
        return entries.reshape(tok_rows, heads_here, head_size).transpose(1, 0, 2)

    q_unit, k_unit, writes, updates, query_key = jax.vmap(prepare)(
        by_head(q_delta), by_head(k_delta), by_head(v_delta), write_rate.T
    )
    transit, carried = jax.vmap(local_pair)(k_unit, writes, updates)
    position = lax.axis_index("seq")
    seq_size = lax.axis_size("seq")
    group = min(4, seq_size)
    rank = position % group

    def moved(value, by, sources):
        pairs = [(i, i + by) for i in sources if 0 <= i + by < seq_size]
        return lax.ppermute(value, "seq", pairs)

    identity = jnp.broadcast_to(jnp.eye(head_size, dtype=jnp.float32), transit.shape)
    before_transit = identity
    before_carried = jnp.zeros_like(carried)
    distance = 1
    while distance < group:
        inside = [i for i in range(seq_size) if i % group + distance < group]
        transit_prev = moved(transit, distance, inside)
        carried_prev = moved(carried, distance, inside)
        has_prev = rank >= distance
        before_carried = jnp.where(
            has_prev, batched_dot(before_transit, carried_prev) + before_carried, before_carried
        )
        before_transit = jnp.where(has_prev, batched_dot(before_transit, transit_prev), before_transit)
        carried_in = jnp.where(has_prev, batched_dot(transit, carried_prev) + carried, carried)
        transit = jnp.where(has_prev, batched_dot(transit, transit_prev), transit)
        carried = carried_in
        distance *= 2
    ends = [i for i in range(seq_size) if i % group == group - 1]
    end_transit, end_carried = transit, carried
    distance = group
    while distance < seq_size:
        final = 2 * distance >= seq_size
        carried_prev = moved(end_carried, distance, ends)
        has_prev = (rank == group - 1) & (position >= distance)
        carried_next = jnp.where(
            has_prev, batched_dot(end_transit, carried_prev) + end_carried, end_carried
        )
        if not final:
            transit_prev = moved(end_transit, distance, ends)
            end_transit = jnp.where(has_prev, batched_dot(end_transit, transit_prev), end_transit)
        end_carried = carried_next
        distance *= 2
    group_in = jnp.zeros_like(carried)
    for hop in range(1, group + 1):
        group_in = group_in + moved(end_carried, hop, ends)
    incoming = batched_dot(before_transit, group_in) + before_carried
    results = jax.vmap(run_blocks)(incoming, q_unit, k_unit, writes, updates, query_key)
    delta_out = (
        results.reshape(heads_here, tok_rows, head_size)
        .transpose(1, 0, 2)
        .reshape(tok_rows, features)
        .astype(jnp.bfloat16)
    )
    shard_reach = WINDOW // tok_rows

    def window_rows(own, lanes):
        lane_length = -(-shard_reach // lanes)
        pieces = []
        for lane in range(lanes):
            first = lane * lane_length + 1
            last = min(shard_reach, (lane + 1) * lane_length)
            piece = shifted(own, "seq", first)
            pieces.append(piece)
            for _ in range(first, last):
                piece = shifted(piece, "seq", 1)
                pieces.append(piece)
        return jnp.concatenate(pieces[::-1] + [own], axis=0)

    rows_all = (window_rows(k_attn, 1), window_rows(delta_out, 2))
    block_rows = min(512, tok_rows)
    first_row = lax.axis_index("seq") * tok_rows
    score_scale = 1.0 / math.sqrt(head_size)

    def attend_block(block_start):
        queries = q_attn.reshape(block_rows, heads_here, head_size)
        near_keys = rows_all[0].reshape(WINDOW + block_rows, heads_here, head_size)
        near_values = rows_all[1].reshape(WINDOW + block_rows, heads_here, head_size)
        scores = (
            jnp.einsum("qhd,khd->hqk", queries, near_keys, preferred_element_type=jnp.float32)
            * score_scale
        )
        q_index = jnp.arange(block_rows)[:, None]
        k_index = jnp.arange(WINDOW + block_rows)[None, :]
        allowed = (
            (k_index > q_index)
            & (k_index <= q_index + WINDOW)
            & (first_row + block_start + k_index >= WINDOW)
        )
        row_top = jnp.max(jnp.where(allowed[None], scores, -1e30), axis=2, keepdims=True)
        exps = jnp.exp(jnp.where(allowed[None], scores - row_top, -1e30))
        weights = (exps / jnp.sum(exps, axis=2, keepdims=True)).astype(jnp.bfloat16)
        mixed_rows = jnp.einsum(
            "hqk,khd->qhd", weights, near_values, preferred_element_type=jnp.float32
        )
        return mixed_rows.reshape(block_rows, features)

    starts = jnp.arange(tok_rows // block_rows) * block_rows
    attended = lax.map(attend_block, starts).reshape(tok_rows, features)
    squares = jnp.sum(attended * attended, axis=1)
    total_sq = lax.psum(squares, "head")
    scale_rows = lax.rsqrt(total_sq / (features * lax.axis_size("head")) + 1e-06)
    normed_out = (attended * out_gain[None, :] * scale_rows[:, None]).astype(jnp.bfloat16)
    return (delta_out, normed_out)


def solution(mesh):
    placed = (
        P("seq", "head"),
        P("seq", "head"),
        P("seq", "head"),
        P("seq", "head"),
        P("seq", "head"),
        P("seq", "head"),
        P("head"),
    )
    return jax.shard_map(
        on_device,
        mesh=mesh,
        in_specs=placed,
        out_specs=(P("seq", "head"), P("seq", "head")),
        check_vma=False,
    )
```

```python
import math

import jax
import jax.numpy as jnp
from jax import lax
from jax.sharding import PartitionSpec as P

GROUP_TOKENS = 64
WINDOW = 2048


highest = lax.Precision.HIGHEST


def shifted(value, axis, by):
    size = lax.axis_size(axis)
    pairs = [(i, i + by) for i in range(size) if 0 <= i + by < size]
    return lax.ppermute(value, axis, pairs)


def unit_rows(entries):
    entries = entries.astype(jnp.float32)
    return entries * lax.rsqrt(jnp.sum(entries * entries, axis=-1, keepdims=True) + 1e-06)


def lower_inverse(below_part):
    length = below_part.shape[-1]
    identity = jnp.eye(length, dtype=jnp.float32)
    result = identity - below_part
    raised = below_part
    doubled = 2
    while doubled < length:
        raised = jnp.einsum("nij,njk->nik", raised, raised, precision=highest)
        result = jnp.einsum("nij,njk->nik", result, identity + raised, precision=highest)
        doubled = doubled * 2
    return result


def prepare(queries, key_rows, values, rate_rows):
    n_groups = queries.shape[0] // GROUP_TOKENS
    q_unit = unit_rows(queries).reshape(n_groups, GROUP_TOKENS, -1)
    k_unit = unit_rows(key_rows).reshape(n_groups, GROUP_TOKENS, -1)
    val_units = values.astype(jnp.float32).reshape(n_groups, GROUP_TOKENS, -1)
    rate_col = rate_rows.reshape(n_groups, GROUP_TOKENS, 1)
    key_inner = jnp.einsum("nik,njk->nij", k_unit, k_unit, precision=highest)
    positions = jnp.arange(GROUP_TOKENS)
    is_below = positions[:, None] > positions[None, :]
    on_or_below = positions[:, None] >= positions[None, :]
    below_part = jnp.where(is_below[None], rate_col * key_inner, 0.0)
    inverse = lower_inverse(below_part)
    writes = jnp.einsum("nij,njk->nik", inverse, rate_col * k_unit, precision=highest)
    updates = jnp.einsum("nij,njk->nik", inverse, rate_col * val_units, precision=highest)
    query_key = jnp.where(
        on_or_below[None], jnp.einsum("nik,njk->nij", q_unit, k_unit, precision=highest), 0.0
    )
    return (q_unit, k_unit, writes, updates, query_key)


def local_pair(k_unit, writes, updates):
    head_size = k_unit.shape[-1]
    identity = jnp.eye(head_size, dtype=jnp.float32)

    def stride(carry, inputs_now):
        transit, carried = carry
        k_block, w_block, u_block = inputs_now
        stepped = identity - jnp.dot(k_block.T, w_block, precision=highest)
        transit = jnp.dot(stepped, transit, precision=highest)
        carried = jnp.dot(stepped, carried, precision=highest) + jnp.dot(
            k_block.T, u_block, precision=highest
        )
        return ((transit, carried), None)

    start_pair = (identity, jnp.zeros((head_size, head_size), jnp.float32))
    (transit, carried), _ = lax.scan(stride, start_pair, (k_unit, writes, updates))
    return (transit, carried)


def advance(carried, inputs_now):
    q_block, k_block, w_block, u_block, cross_block = inputs_now
    corrected = u_block - jnp.dot(w_block, carried, precision=highest)
    result_now = jnp.dot(q_block, carried, precision=highest) + jnp.dot(
        cross_block, corrected, precision=highest
    )
    return (carried + jnp.dot(k_block.T, corrected, precision=highest), result_now)


def run_blocks(carried_in, q_unit, k_unit, writes, updates, query_key):
    _, results = lax.scan(advance, carried_in, (q_unit, k_unit, writes, updates, query_key))
    return results


def batched_dot(left, right):
    return jnp.einsum("hij,hjk->hik", left, right, precision=highest)


def on_device(q_delta, k_delta, v_delta, write_rate, q_attn, k_attn, out_gain):
    tok_rows, features = q_delta.shape
    heads_here = write_rate.shape[1]
    head_size = features // heads_here

    def by_head(entries):
        return entries.reshape(tok_rows, heads_here, head_size).transpose(1, 0, 2)

    q_unit, k_unit, writes, updates, query_key = jax.vmap(prepare)(
        by_head(q_delta), by_head(k_delta), by_head(v_delta), write_rate.T
    )
    transit, carried = jax.vmap(local_pair)(k_unit, writes, updates)
    position = lax.axis_index("seq")
    seq_size = lax.axis_size("seq")
    group = min(4, seq_size)
    rank = position % group

    def moved(value, by, sources):
        pairs = [(i, i + by) for i in sources if 0 <= i + by < seq_size]
        return lax.ppermute(value, "seq", pairs)

    identity = jnp.broadcast_to(jnp.eye(head_size, dtype=jnp.float32), transit.shape)
    before_transit = identity
    before_carried = jnp.zeros_like(carried)
    distance = 1
    while distance < group:
        inside = [i for i in range(seq_size) if i % group + distance < group]
        transit_prev = moved(transit, distance, inside)
        carried_prev = moved(carried, distance, inside)
        has_prev = rank >= distance
        before_carried = jnp.where(
            has_prev, batched_dot(before_transit, carried_prev) + before_carried, before_carried
        )
        before_transit = jnp.where(has_prev, batched_dot(before_transit, transit_prev), before_transit)
        carried_in = jnp.where(has_prev, batched_dot(transit, carried_prev) + carried, carried)
        transit = jnp.where(has_prev, batched_dot(transit, transit_prev), transit)
        carried = carried_in
        distance *= 2
    ends = [i for i in range(seq_size) if i % group == group - 1]
    end_transit, end_carried = transit, carried
    distance = group
    while distance < seq_size:
        final = 2 * distance >= seq_size
        carried_prev = moved(end_carried, distance, ends)
        has_prev = (rank == group - 1) & (position >= distance)
        carried_next = jnp.where(
            has_prev, batched_dot(end_transit, carried_prev) + end_carried, end_carried
        )
        if not final:
            transit_prev = moved(end_transit, distance, ends)
            end_transit = jnp.where(has_prev, batched_dot(end_transit, transit_prev), end_transit)
        end_carried = carried_next
        distance *= 2
    group_in = jnp.zeros_like(carried)
    for hop in range(1, group + 1):
        group_in = group_in + moved(end_carried, hop, ends)
    incoming = batched_dot(before_transit, group_in) + before_carried
    results = jax.vmap(run_blocks)(incoming, q_unit, k_unit, writes, updates, query_key)
    delta_out = (
        results.reshape(heads_here, tok_rows, head_size)
        .transpose(1, 0, 2)
        .reshape(tok_rows, features)
        .astype(jnp.bfloat16)
    )
    shard_reach = WINDOW // tok_rows

    def window_rows(own, lanes):
        lane_length = -(-shard_reach // lanes)
        pieces = []
        for lane in range(lanes):
            first = lane * lane_length + 1
            last = min(shard_reach, (lane + 1) * lane_length)
            piece = shifted(own, "seq", first)
            pieces.append(piece)
            for _ in range(first, last):
                piece = shifted(piece, "seq", 1)
                pieces.append(piece)
        return jnp.concatenate(pieces[::-1] + [own], axis=0)

    rows_all = (window_rows(k_attn, 2), window_rows(delta_out, 2))
    block_rows = min(512, tok_rows)
    first_row = lax.axis_index("seq") * tok_rows
    score_scale = 1.0 / math.sqrt(head_size)

    def attend_block(block_start):
        queries = q_attn.reshape(block_rows, heads_here, head_size)
        near_keys = rows_all[0].reshape(WINDOW + block_rows, heads_here, head_size)
        near_values = rows_all[1].reshape(WINDOW + block_rows, heads_here, head_size)
        scores = (
            jnp.einsum("qhd,khd->hqk", queries, near_keys, preferred_element_type=jnp.float32)
            * score_scale
        )
        q_index = jnp.arange(block_rows)[:, None]
        k_index = jnp.arange(WINDOW + block_rows)[None, :]
        allowed = (
            (k_index > q_index)
            & (k_index <= q_index + WINDOW)
            & (first_row + block_start + k_index >= WINDOW)
        )
        row_top = jnp.max(jnp.where(allowed[None], scores, -1e30), axis=2, keepdims=True)
        exps = jnp.exp(jnp.where(allowed[None], scores - row_top, -1e30))
        weights = (exps / jnp.sum(exps, axis=2, keepdims=True)).astype(jnp.bfloat16)
        mixed_rows = jnp.einsum(
            "hqk,khd->qhd", weights, near_values, preferred_element_type=jnp.float32
        )
        return mixed_rows.reshape(block_rows, features)

    starts = jnp.arange(tok_rows // block_rows) * block_rows
    attended = lax.map(attend_block, starts).reshape(tok_rows, features)
    squares = jnp.sum(attended * attended, axis=1)
    total_sq = lax.psum(squares, "head")
    scale_rows = lax.rsqrt(total_sq / (features * lax.axis_size("head")) + 1e-06)
    normed_out = (attended * out_gain[None, :] * scale_rows[:, None]).astype(jnp.bfloat16)
    return (delta_out, normed_out)


def solution(mesh):
    placed = (
        P("seq", "head"),
        P("seq", "head"),
        P("seq", "head"),
        P("seq", "head"),
        P("seq", "head"),
        P("seq", "head"),
        P("head"),
    )
    return jax.shard_map(
        on_device,
        mesh=mesh,
        in_specs=placed,
        out_specs=(P("seq", "head"), P("seq", "head")),
        check_vma=False,
    )
```

```python
import math

import jax
import jax.numpy as jnp
from jax import lax
from jax.sharding import PartitionSpec as P

GROUP_TOKENS = 64
WINDOW = 2048


highest = lax.Precision.HIGHEST


def shifted(value, axis, by):
    size = lax.axis_size(axis)
    pairs = [(i, i + by) for i in range(size) if 0 <= i + by < size]
    return lax.ppermute(value, axis, pairs)


def unit_rows(entries):
    entries = entries.astype(jnp.float32)
    return entries * lax.rsqrt(jnp.sum(entries * entries, axis=-1, keepdims=True) + 1e-06)


def lower_inverse(below_part):
    length = below_part.shape[-1]
    identity = jnp.eye(length, dtype=jnp.float32)
    result = identity - below_part
    raised = below_part
    doubled = 2
    while doubled < length:
        raised = jnp.einsum("nij,njk->nik", raised, raised, precision=highest)
        result = jnp.einsum("nij,njk->nik", result, identity + raised, precision=highest)
        doubled = doubled * 2
    return result


def prepare(queries, key_rows, values, rate_rows):
    n_groups = queries.shape[0] // GROUP_TOKENS
    q_unit = unit_rows(queries).reshape(n_groups, GROUP_TOKENS, -1)
    k_unit = unit_rows(key_rows).reshape(n_groups, GROUP_TOKENS, -1)
    val_units = values.astype(jnp.float32).reshape(n_groups, GROUP_TOKENS, -1)
    rate_col = rate_rows.reshape(n_groups, GROUP_TOKENS, 1)
    key_inner = jnp.einsum("nik,njk->nij", k_unit, k_unit, precision=highest)
    positions = jnp.arange(GROUP_TOKENS)
    is_below = positions[:, None] > positions[None, :]
    on_or_below = positions[:, None] >= positions[None, :]
    below_part = jnp.where(is_below[None], rate_col * key_inner, 0.0)
    inverse = lower_inverse(below_part)
    writes = jnp.einsum("nij,njk->nik", inverse, rate_col * k_unit, precision=highest)
    updates = jnp.einsum("nij,njk->nik", inverse, rate_col * val_units, precision=highest)
    query_key = jnp.where(
        on_or_below[None], jnp.einsum("nik,njk->nij", q_unit, k_unit, precision=highest), 0.0
    )
    return (q_unit, k_unit, writes, updates, query_key)


def local_pair(k_unit, writes, updates):
    head_size = k_unit.shape[-1]
    identity = jnp.eye(head_size, dtype=jnp.float32)

    def stride(carry, inputs_now):
        transit, carried = carry
        k_block, w_block, u_block = inputs_now
        stepped = identity - jnp.dot(k_block.T, w_block, precision=highest)
        transit = jnp.dot(stepped, transit, precision=highest)
        carried = jnp.dot(stepped, carried, precision=highest) + jnp.dot(
            k_block.T, u_block, precision=highest
        )
        return ((transit, carried), None)

    start_pair = (identity, jnp.zeros((head_size, head_size), jnp.float32))
    (transit, carried), _ = lax.scan(stride, start_pair, (k_unit, writes, updates))
    return (transit, carried)


def advance(carried, inputs_now):
    q_block, k_block, w_block, u_block, cross_block = inputs_now
    corrected = u_block - jnp.dot(w_block, carried, precision=highest)
    result_now = jnp.dot(q_block, carried, precision=highest) + jnp.dot(
        cross_block, corrected, precision=highest
    )
    return (carried + jnp.dot(k_block.T, corrected, precision=highest), result_now)


def run_blocks(carried_in, q_unit, k_unit, writes, updates, query_key):
    _, results = lax.scan(advance, carried_in, (q_unit, k_unit, writes, updates, query_key))
    return results


def batched_dot(left, right):
    return jnp.einsum("hij,hjk->hik", left, right, precision=highest)


def on_device(q_delta, k_delta, v_delta, write_rate, q_attn, k_attn, out_gain):
    tok_rows, features = q_delta.shape
    heads_here = write_rate.shape[1]
    head_size = features // heads_here

    def by_head(entries):
        return entries.reshape(tok_rows, heads_here, head_size).transpose(1, 0, 2)

    q_unit, k_unit, writes, updates, query_key = jax.vmap(prepare)(
        by_head(q_delta), by_head(k_delta), by_head(v_delta), write_rate.T
    )
    transit, carried = jax.vmap(local_pair)(k_unit, writes, updates)
    position = lax.axis_index("seq")
    seq_size = lax.axis_size("seq")
    group = min(4, seq_size)
    rank = position % group

    def moved(value, by, sources):
        pairs = [(i, i + by) for i in sources if 0 <= i + by < seq_size]
        return lax.ppermute(value, "seq", pairs)

    identity = jnp.broadcast_to(jnp.eye(head_size, dtype=jnp.float32), transit.shape)
    before_transit = identity
    before_carried = jnp.zeros_like(carried)
    distance = 1
    while distance < group:
        inside = [i for i in range(seq_size) if i % group + distance < group]
        transit_prev = moved(transit, distance, inside)
        carried_prev = moved(carried, distance, inside)
        has_prev = rank >= distance
        before_carried = jnp.where(
            has_prev, batched_dot(before_transit, carried_prev) + before_carried, before_carried
        )
        before_transit = jnp.where(has_prev, batched_dot(before_transit, transit_prev), before_transit)
        carried_in = jnp.where(has_prev, batched_dot(transit, carried_prev) + carried, carried)
        transit = jnp.where(has_prev, batched_dot(transit, transit_prev), transit)
        carried = carried_in
        distance *= 2
    ends = [i for i in range(seq_size) if i % group == group - 1]
    end_transit, end_carried = transit, carried
    distance = group
    while distance < seq_size:
        final = 2 * distance >= seq_size
        carried_prev = moved(end_carried, distance, ends)
        has_prev = (rank == group - 1) & (position >= distance)
        carried_next = jnp.where(
            has_prev, batched_dot(end_transit, carried_prev) + end_carried, end_carried
        )
        if not final:
            transit_prev = moved(end_transit, distance, ends)
            end_transit = jnp.where(has_prev, batched_dot(end_transit, transit_prev), end_transit)
        end_carried = carried_next
        distance *= 2
    group_in = jnp.zeros_like(carried)
    for hop in range(1, group + 1):
        group_in = group_in + moved(end_carried, hop, ends)
    incoming = batched_dot(before_transit, group_in) + before_carried
    results = jax.vmap(run_blocks)(incoming, q_unit, k_unit, writes, updates, query_key)
    delta_out = (
        results.reshape(heads_here, tok_rows, head_size)
        .transpose(1, 0, 2)
        .reshape(tok_rows, features)
        .astype(jnp.bfloat16)
    )
    shard_reach = WINDOW // tok_rows

    def window_rows(own, lanes):
        lane_length = -(-shard_reach // lanes)
        pieces = []
        for lane in range(lanes):
            first = lane * lane_length + 1
            last = min(shard_reach, (lane + 1) * lane_length)
            piece = shifted(own, "seq", first)
            pieces.append(piece)
            for _ in range(first, last):
                piece = shifted(piece, "seq", 1)
                pieces.append(piece)
        return jnp.concatenate(pieces[::-1] + [own], axis=0)

    rows_all = (window_rows(k_attn, 1), window_rows(delta_out, 2))
    block_rows = min(512, tok_rows)
    first_row = lax.axis_index("seq") * tok_rows
    score_scale = 1.0 / math.sqrt(head_size)

    def attend_block(block_start):
        queries = q_attn.reshape(block_rows, heads_here, head_size)
        near_keys = rows_all[0].reshape(WINDOW + block_rows, heads_here, head_size)
        near_values = rows_all[1].reshape(WINDOW + block_rows, heads_here, head_size)
        scores = (
            jnp.einsum("qhd,khd->hqk", queries, near_keys, preferred_element_type=jnp.float32)
            * score_scale
        )
        q_index = jnp.arange(block_rows)[:, None]
        k_index = jnp.arange(WINDOW + block_rows)[None, :]
        allowed = (
            (k_index > q_index)
            & (k_index <= q_index + WINDOW)
            & (first_row + block_start + k_index >= WINDOW)
        )
        row_top = jnp.max(jnp.where(allowed[None], scores, -1e30), axis=2, keepdims=True)
        exps = jnp.exp(jnp.where(allowed[None], scores - row_top, -1e30))
        weights = (exps / jnp.sum(exps, axis=2, keepdims=True)).astype(jnp.bfloat16)
        mixed_rows = jnp.einsum(
            "hqk,khd->qhd", weights, near_values, preferred_element_type=jnp.float32
        )
        return mixed_rows.reshape(block_rows, features)

    starts = jnp.arange(tok_rows // block_rows) * block_rows
    attended = lax.map(attend_block, starts).reshape(tok_rows, features)
    squares = jnp.sum(attended * attended, axis=1)
    head_count = lax.axis_size("head")
    pair_sq = squares + lax.ppermute(squares, "head", [(i, i ^ 1) for i in range(head_count)])
    total_sq = pair_sq
    for offset in range(2, head_count, 2):
        pairs = [(i, (i + offset) % head_count) for i in range(head_count)]
        total_sq = total_sq + lax.ppermute(pair_sq, "head", pairs)
    scale_rows = lax.rsqrt(total_sq / (features * lax.axis_size("head")) + 1e-06)
    normed_out = (attended * out_gain[None, :] * scale_rows[:, None]).astype(jnp.bfloat16)
    return (delta_out, normed_out)


def solution(mesh):
    placed = (
        P("seq", "head"),
        P("seq", "head"),
        P("seq", "head"),
        P("seq", "head"),
        P("seq", "head"),
        P("seq", "head"),
        P("head"),
    )
    return jax.shard_map(
        on_device,
        mesh=mesh,
        in_specs=placed,
        out_specs=(P("seq", "head"), P("seq", "head")),
        check_vma=False,
    )
```

```python
import math

import jax
import jax.numpy as jnp
from jax import lax
from jax.sharding import PartitionSpec as P

GROUP_TOKENS = 64
WINDOW = 2048


highest = lax.Precision.HIGHEST


def shifted(value, axis, by):
    size = lax.axis_size(axis)
    pairs = [(i, i + by) for i in range(size) if 0 <= i + by < size]
    return lax.ppermute(value, axis, pairs)


def unit_rows(entries):
    entries = entries.astype(jnp.float32)
    return entries * lax.rsqrt(jnp.sum(entries * entries, axis=-1, keepdims=True) + 1e-06)


def lower_inverse(below_part):
    length = below_part.shape[-1]
    identity = jnp.eye(length, dtype=jnp.float32)
    result = identity - below_part
    raised = below_part
    doubled = 2
    while doubled < length:
        raised = jnp.einsum("nij,njk->nik", raised, raised, precision=highest)
        result = jnp.einsum("nij,njk->nik", result, identity + raised, precision=highest)
        doubled = doubled * 2
    return result


def prepare(queries, key_rows, values, rate_rows):
    n_groups = queries.shape[0] // GROUP_TOKENS
    q_unit = unit_rows(queries).reshape(n_groups, GROUP_TOKENS, -1)
    k_unit = unit_rows(key_rows).reshape(n_groups, GROUP_TOKENS, -1)
    val_units = values.astype(jnp.float32).reshape(n_groups, GROUP_TOKENS, -1)
    rate_col = rate_rows.reshape(n_groups, GROUP_TOKENS, 1)
    key_inner = jnp.einsum("nik,njk->nij", k_unit, k_unit, precision=highest)
    positions = jnp.arange(GROUP_TOKENS)
    is_below = positions[:, None] > positions[None, :]
    on_or_below = positions[:, None] >= positions[None, :]
    below_part = jnp.where(is_below[None], rate_col * key_inner, 0.0)
    inverse = lower_inverse(below_part)
    writes = jnp.einsum("nij,njk->nik", inverse, rate_col * k_unit, precision=highest)
    updates = jnp.einsum("nij,njk->nik", inverse, rate_col * val_units, precision=highest)
    query_key = jnp.where(
        on_or_below[None], jnp.einsum("nik,njk->nij", q_unit, k_unit, precision=highest), 0.0
    )
    return (q_unit, k_unit, writes, updates, query_key)


def local_pair(k_unit, writes, updates):
    head_size = k_unit.shape[-1]
    identity = jnp.eye(head_size, dtype=jnp.float32)

    def stride(carry, inputs_now):
        transit, carried = carry
        k_block, w_block, u_block = inputs_now
        stepped = identity - jnp.dot(k_block.T, w_block, precision=highest)
        transit = jnp.dot(stepped, transit, precision=highest)
        carried = jnp.dot(stepped, carried, precision=highest) + jnp.dot(
            k_block.T, u_block, precision=highest
        )
        return ((transit, carried), None)

    start_pair = (identity, jnp.zeros((head_size, head_size), jnp.float32))
    (transit, carried), _ = lax.scan(stride, start_pair, (k_unit, writes, updates))
    return (transit, carried)


def local_affine(q_unit, k_unit, writes, updates, query_key):
    n_blocks, _, head_size = k_unit.shape
    identity = jnp.eye(head_size, dtype=jnp.float32)
    key_cols = jnp.swapaxes(k_unit, -1, -2)
    stepped = identity - jnp.einsum("nij,njk->nik", key_cols, writes, precision=highest)
    written = jnp.einsum("nij,njk->nik", key_cols, updates, precision=highest)
    transit_list = [identity]
    carried_list = [jnp.zeros_like(identity)]
    for block in range(n_blocks):
        transit_list.append(jnp.dot(stepped[block], transit_list[-1], precision=highest))
        carried_list.append(
            jnp.dot(stepped[block], carried_list[-1], precision=highest) + written[block]
        )
    transit_before = jnp.stack(transit_list[:-1])
    carried_before = jnp.stack(carried_list[:-1])
    reading = q_unit - jnp.einsum("nij,njk->nik", query_key, writes, precision=highest)
    slope = jnp.einsum("nij,njk->nik", reading, transit_before, precision=highest)
    offset = jnp.einsum("nij,njk->nik", reading, carried_before, precision=highest) + jnp.einsum(
        "nij,njk->nik", query_key, updates, precision=highest
    )
    rows = n_blocks * k_unit.shape[1]
    return (
        transit_list[-1],
        carried_list[-1],
        slope.reshape(rows, head_size),
        offset.reshape(rows, head_size),
    )


def advance(carried, inputs_now):
    q_block, k_block, w_block, u_block, cross_block = inputs_now
    corrected = u_block - jnp.dot(w_block, carried, precision=highest)
    result_now = jnp.dot(q_block, carried, precision=highest) + jnp.dot(
        cross_block, corrected, precision=highest
    )
    return (carried + jnp.dot(k_block.T, corrected, precision=highest), result_now)


def run_blocks(carried_in, q_unit, k_unit, writes, updates, query_key):
    _, results = lax.scan(advance, carried_in, (q_unit, k_unit, writes, updates, query_key))
    return results


def batched_dot(left, right):
    return jnp.einsum("hij,hjk->hik", left, right, precision=highest)


def on_device(q_delta, k_delta, v_delta, write_rate, q_attn, k_attn, out_gain):
    tok_rows, features = q_delta.shape
    heads_here = write_rate.shape[1]
    head_size = features // heads_here

    def by_head(entries):
        return entries.reshape(tok_rows, heads_here, head_size).transpose(1, 0, 2)

    q_unit, k_unit, writes, updates, query_key = jax.vmap(prepare)(
        by_head(q_delta), by_head(k_delta), by_head(v_delta), write_rate.T
    )
    transit, carried, slope, offset = jax.vmap(local_affine)(
        q_unit, k_unit, writes, updates, query_key
    )
    position = lax.axis_index("seq")
    seq_size = lax.axis_size("seq")
    group = min(4, seq_size)
    rank = position % group

    def moved(value, by, sources):
        pairs = [(i, i + by) for i in sources if 0 <= i + by < seq_size]
        return lax.ppermute(value, "seq", pairs)

    identity = jnp.broadcast_to(jnp.eye(head_size, dtype=jnp.float32), transit.shape)
    before_transit = identity
    before_carried = jnp.zeros_like(carried)
    distance = 1
    while distance < group:
        inside = [i for i in range(seq_size) if i % group + distance < group]
        transit_prev = moved(transit, distance, inside)
        carried_prev = moved(carried, distance, inside)
        has_prev = rank >= distance
        before_carried = jnp.where(
            has_prev, batched_dot(before_transit, carried_prev) + before_carried, before_carried
        )
        before_transit = jnp.where(has_prev, batched_dot(before_transit, transit_prev), before_transit)
        carried_in = jnp.where(has_prev, batched_dot(transit, carried_prev) + carried, carried)
        transit = jnp.where(has_prev, batched_dot(transit, transit_prev), transit)
        carried = carried_in
        distance *= 2
    ends = [i for i in range(seq_size) if i % group == group - 1]
    end_transit, end_carried = transit, carried
    distance = group
    while distance < seq_size:
        final = 2 * distance >= seq_size
        carried_prev = moved(end_carried, distance, ends)
        has_prev = (rank == group - 1) & (position >= distance)
        carried_next = jnp.where(
            has_prev, batched_dot(end_transit, carried_prev) + end_carried, end_carried
        )
        if not final:
            transit_prev = moved(end_transit, distance, ends)
            end_transit = jnp.where(has_prev, batched_dot(end_transit, transit_prev), end_transit)
        end_carried = carried_next
        distance *= 2
    group_in = jnp.zeros_like(carried)
    for hop in range(1, group + 1):
        group_in = group_in + moved(end_carried, hop, ends)
    offset = offset + batched_dot(slope, before_carried)
    slope = batched_dot(slope, before_transit)
    results = batched_dot(slope, group_in) + offset
    delta_out = (
        results.reshape(heads_here, tok_rows, head_size)
        .transpose(1, 0, 2)
        .reshape(tok_rows, features)
        .astype(jnp.bfloat16)
    )
    shard_reach = WINDOW // tok_rows

    def window_rows(own, lanes):
        lane_length = -(-shard_reach // lanes)
        pieces = []
        for lane in range(lanes):
            first = lane * lane_length + 1
            last = min(shard_reach, (lane + 1) * lane_length)
            piece = shifted(own, "seq", first)
            pieces.append(piece)
            for _ in range(first, last):
                piece = shifted(piece, "seq", 1)
                pieces.append(piece)
        return jnp.concatenate(pieces[::-1] + [own], axis=0)

    rows_all = (window_rows(k_attn, 1), window_rows(delta_out, 2))
    block_rows = min(512, tok_rows)
    first_row = lax.axis_index("seq") * tok_rows
    score_scale = 1.0 / math.sqrt(head_size)

    def attend_block(block_start):
        queries = q_attn.reshape(block_rows, heads_here, head_size)
        near_keys = rows_all[0].reshape(WINDOW + block_rows, heads_here, head_size)
        near_values = rows_all[1].reshape(WINDOW + block_rows, heads_here, head_size)
        scores = (
            jnp.einsum("qhd,khd->hqk", queries, near_keys, preferred_element_type=jnp.float32)
            * score_scale
        )
        q_index = jnp.arange(block_rows)[:, None]
        k_index = jnp.arange(WINDOW + block_rows)[None, :]
        allowed = (
            (k_index > q_index)
            & (k_index <= q_index + WINDOW)
            & (first_row + block_start + k_index >= WINDOW)
        )
        row_top = jnp.max(jnp.where(allowed[None], scores, -1e30), axis=2, keepdims=True)
        exps = jnp.exp(jnp.where(allowed[None], scores - row_top, -1e30))
        weights = (exps / jnp.sum(exps, axis=2, keepdims=True)).astype(jnp.bfloat16)
        mixed_rows = jnp.einsum(
            "hqk,khd->qhd", weights, near_values, preferred_element_type=jnp.float32
        )
        return mixed_rows.reshape(block_rows, features)

    starts = jnp.arange(tok_rows // block_rows) * block_rows
    attended = lax.map(attend_block, starts).reshape(tok_rows, features)
    squares = jnp.sum(attended * attended, axis=1)
    total_sq = lax.psum(squares, "head")
    scale_rows = lax.rsqrt(total_sq / (features * lax.axis_size("head")) + 1e-06)
    normed_out = (attended * out_gain[None, :] * scale_rows[:, None]).astype(jnp.bfloat16)
    return (delta_out, normed_out)


def solution(mesh):
    placed = (
        P("seq", "head"),
        P("seq", "head"),
        P("seq", "head"),
        P("seq", "head"),
        P("seq", "head"),
        P("seq", "head"),
        P("head"),
    )
    return jax.shard_map(
        on_device,
        mesh=mesh,
        in_specs=placed,
        out_specs=(P("seq", "head"), P("seq", "head")),
        check_vma=False,
    )
```

```python
import math

import jax
import jax.numpy as jnp
from jax import lax
from jax.sharding import PartitionSpec as P

GROUP_TOKENS = 64
WINDOW = 2048


highest = lax.Precision.HIGHEST


def shifted(value, axis, by):
    size = lax.axis_size(axis)
    pairs = [(i, i + by) for i in range(size) if 0 <= i + by < size]
    return lax.ppermute(value, axis, pairs)


def unit_rows(entries):
    entries = entries.astype(jnp.float32)
    return entries * lax.rsqrt(jnp.sum(entries * entries, axis=-1, keepdims=True) + 1e-06)


def lower_inverse(below_part):
    length = below_part.shape[-1]
    identity = jnp.eye(length, dtype=jnp.float32)
    result = identity - below_part
    raised = below_part
    doubled = 2
    while doubled < length:
        raised = jnp.einsum("nij,njk->nik", raised, raised, precision=highest)
        result = jnp.einsum("nij,njk->nik", result, identity + raised, precision=highest)
        doubled = doubled * 2
    return result


def prepare(queries, key_rows, values, rate_rows):
    n_groups = queries.shape[0] // GROUP_TOKENS
    q_unit = unit_rows(queries).reshape(n_groups, GROUP_TOKENS, -1)
    k_unit = unit_rows(key_rows).reshape(n_groups, GROUP_TOKENS, -1)
    val_units = values.astype(jnp.float32).reshape(n_groups, GROUP_TOKENS, -1)
    rate_col = rate_rows.reshape(n_groups, GROUP_TOKENS, 1)
    key_inner = jnp.einsum("nik,njk->nij", k_unit, k_unit, precision=highest)
    positions = jnp.arange(GROUP_TOKENS)
    is_below = positions[:, None] > positions[None, :]
    on_or_below = positions[:, None] >= positions[None, :]
    below_part = jnp.where(is_below[None], rate_col * key_inner, 0.0)
    inverse = lower_inverse(below_part)
    writes = jnp.einsum("nij,njk->nik", inverse, rate_col * k_unit, precision=highest)
    updates = jnp.einsum("nij,njk->nik", inverse, rate_col * val_units, precision=highest)
    query_key = jnp.where(
        on_or_below[None], jnp.einsum("nik,njk->nij", q_unit, k_unit, precision=highest), 0.0
    )
    return (q_unit, k_unit, writes, updates, query_key)


def local_pair(k_unit, writes, updates):
    head_size = k_unit.shape[-1]
    identity = jnp.eye(head_size, dtype=jnp.float32)

    def stride(carry, inputs_now):
        transit, carried = carry
        k_block, w_block, u_block = inputs_now
        stepped = identity - jnp.dot(k_block.T, w_block, precision=highest)
        transit = jnp.dot(stepped, transit, precision=highest)
        carried = jnp.dot(stepped, carried, precision=highest) + jnp.dot(
            k_block.T, u_block, precision=highest
        )
        return ((transit, carried), None)

    start_pair = (identity, jnp.zeros((head_size, head_size), jnp.float32))
    (transit, carried), _ = lax.scan(stride, start_pair, (k_unit, writes, updates))
    return (transit, carried)


def local_affine(q_unit, k_unit, writes, updates, query_key):
    n_blocks, _, head_size = k_unit.shape
    identity = jnp.eye(head_size, dtype=jnp.float32)
    key_cols = jnp.swapaxes(k_unit, -1, -2)
    stepped = identity - jnp.einsum("nij,njk->nik", key_cols, writes, precision=highest)
    written = jnp.einsum("nij,njk->nik", key_cols, updates, precision=highest)
    transit_list = [identity]
    carried_list = [jnp.zeros_like(identity)]
    for block in range(n_blocks):
        transit_list.append(jnp.dot(stepped[block], transit_list[-1], precision=highest))
        carried_list.append(
            jnp.dot(stepped[block], carried_list[-1], precision=highest) + written[block]
        )
    transit_before = jnp.stack(transit_list[:-1])
    carried_before = jnp.stack(carried_list[:-1])
    reading = q_unit - jnp.einsum("nij,njk->nik", query_key, writes, precision=highest)
    slope = jnp.einsum("nij,njk->nik", reading, transit_before, precision=highest)
    offset = jnp.einsum("nij,njk->nik", reading, carried_before, precision=highest) + jnp.einsum(
        "nij,njk->nik", query_key, updates, precision=highest
    )
    rows = n_blocks * k_unit.shape[1]
    return (
        transit_list[-1],
        carried_list[-1],
        slope.reshape(rows, head_size),
        offset.reshape(rows, head_size),
    )


def advance(carried, inputs_now):
    q_block, k_block, w_block, u_block, cross_block = inputs_now
    corrected = u_block - jnp.dot(w_block, carried, precision=highest)
    result_now = jnp.dot(q_block, carried, precision=highest) + jnp.dot(
        cross_block, corrected, precision=highest
    )
    return (carried + jnp.dot(k_block.T, corrected, precision=highest), result_now)


def run_blocks(carried_in, q_unit, k_unit, writes, updates, query_key):
    _, results = lax.scan(advance, carried_in, (q_unit, k_unit, writes, updates, query_key))
    return results


def batched_dot(left, right):
    return jnp.einsum("hij,hjk->hik", left, right, precision=highest)


def on_device(q_delta, k_delta, v_delta, write_rate, q_attn, k_attn, out_gain):
    tok_rows, features = q_delta.shape
    heads_here = write_rate.shape[1]
    head_size = features // heads_here

    def by_head(entries):
        return entries.reshape(tok_rows, heads_here, head_size).transpose(1, 0, 2)

    q_unit, k_unit, writes, updates, query_key = jax.vmap(prepare)(
        by_head(q_delta), by_head(k_delta), by_head(v_delta), write_rate.T
    )
    transit, carried, slope, offset = jax.vmap(local_affine)(
        q_unit, k_unit, writes, updates, query_key
    )
    position = lax.axis_index("seq")
    seq_size = lax.axis_size("seq")
    group = min(4, seq_size)
    rank = position % group

    def moved(value, by, sources):
        pairs = [(i, i + by) for i in sources if 0 <= i + by < seq_size]
        return lax.ppermute(value, "seq", pairs)

    identity = jnp.broadcast_to(jnp.eye(head_size, dtype=jnp.float32), transit.shape)
    before_transit = identity
    before_carried = jnp.zeros_like(carried)
    distance = 1
    while distance < group:
        inside = [i for i in range(seq_size) if i % group + distance < group]
        transit_prev = moved(transit, distance, inside)
        carried_prev = moved(carried, distance, inside)
        has_prev = rank >= distance
        before_carried = jnp.where(
            has_prev, batched_dot(before_transit, carried_prev) + before_carried, before_carried
        )
        before_transit = jnp.where(has_prev, batched_dot(before_transit, transit_prev), before_transit)
        carried_in = jnp.where(has_prev, batched_dot(transit, carried_prev) + carried, carried)
        transit = jnp.where(has_prev, batched_dot(transit, transit_prev), transit)
        carried = carried_in
        distance *= 2
    shard_reach = WINDOW // tok_rows

    def window_rows(own, lanes):
        lane_length = -(-shard_reach // lanes)
        pieces = []
        for lane in range(lanes):
            first = lane * lane_length + 1
            last = min(shard_reach, (lane + 1) * lane_length)
            piece = shifted(own, "seq", first)
            pieces.append(piece)
            for _ in range(first, last):
                piece = shifted(piece, "seq", 1)
                pieces.append(piece)
        return jnp.concatenate(pieces[::-1] + [own], axis=0)

    key_rows = window_rows(k_attn, 1)
    transit, carried, key_rows = lax.optimization_barrier((transit, carried, key_rows))
    ends = [i for i in range(seq_size) if i % group == group - 1]
    end_transit, end_carried = transit, carried
    distance = group
    while distance < seq_size:
        final = 2 * distance >= seq_size
        carried_prev = moved(end_carried, distance, ends)
        has_prev = (rank == group - 1) & (position >= distance)
        carried_next = jnp.where(
            has_prev, batched_dot(end_transit, carried_prev) + end_carried, end_carried
        )
        if not final:
            transit_prev = moved(end_transit, distance, ends)
            end_transit = jnp.where(has_prev, batched_dot(end_transit, transit_prev), end_transit)
        end_carried = carried_next
        distance *= 2
    group_in = jnp.zeros_like(carried)
    for hop in range(1, group + 1):
        group_in = group_in + moved(end_carried, hop, ends)
    offset = offset + batched_dot(slope, before_carried)
    slope = batched_dot(slope, before_transit)
    results = batched_dot(slope, group_in) + offset
    delta_out = (
        results.reshape(heads_here, tok_rows, head_size)
        .transpose(1, 0, 2)
        .reshape(tok_rows, features)
        .astype(jnp.bfloat16)
    )
    rows_all = (key_rows, window_rows(delta_out, 2))
    block_rows = min(512, tok_rows)
    first_row = lax.axis_index("seq") * tok_rows
    score_scale = 1.0 / math.sqrt(head_size)

    def attend_block(block_start):
        queries = q_attn.reshape(block_rows, heads_here, head_size)
        near_keys = rows_all[0].reshape(WINDOW + block_rows, heads_here, head_size)
        near_values = rows_all[1].reshape(WINDOW + block_rows, heads_here, head_size)
        scores = (
            jnp.einsum("qhd,khd->hqk", queries, near_keys, preferred_element_type=jnp.float32)
            * score_scale
        )
        q_index = jnp.arange(block_rows)[:, None]
        k_index = jnp.arange(WINDOW + block_rows)[None, :]
        allowed = (
            (k_index > q_index)
            & (k_index <= q_index + WINDOW)
            & (first_row + block_start + k_index >= WINDOW)
        )
        row_top = jnp.max(jnp.where(allowed[None], scores, -1e30), axis=2, keepdims=True)
        exps = jnp.exp(jnp.where(allowed[None], scores - row_top, -1e30))
        weights = (exps / jnp.sum(exps, axis=2, keepdims=True)).astype(jnp.bfloat16)
        mixed_rows = jnp.einsum(
            "hqk,khd->qhd", weights, near_values, preferred_element_type=jnp.float32
        )
        return mixed_rows.reshape(block_rows, features)

    starts = jnp.arange(tok_rows // block_rows) * block_rows
    attended = lax.map(attend_block, starts).reshape(tok_rows, features)
    squares = jnp.sum(attended * attended, axis=1)
    total_sq = lax.psum(squares, "head")
    scale_rows = lax.rsqrt(total_sq / (features * lax.axis_size("head")) + 1e-06)
    normed_out = (attended * out_gain[None, :] * scale_rows[:, None]).astype(jnp.bfloat16)
    return (delta_out, normed_out)


def solution(mesh):
    placed = (
        P("seq", "head"),
        P("seq", "head"),
        P("seq", "head"),
        P("seq", "head"),
        P("seq", "head"),
        P("seq", "head"),
        P("head"),
    )
    return jax.shard_map(
        on_device,
        mesh=mesh,
        in_specs=placed,
        out_specs=(P("seq", "head"), P("seq", "head")),
        check_vma=False,
    )
```

```python
import math

import jax
import jax.numpy as jnp
from jax import lax
from jax.sharding import PartitionSpec as P

GROUP_TOKENS = 64
WINDOW = 2048


highest = lax.Precision.HIGHEST


def shifted(value, axis, by):
    size = lax.axis_size(axis)
    pairs = [(i, i + by) for i in range(size) if 0 <= i + by < size]
    return lax.ppermute(value, axis, pairs)


def unit_rows(entries):
    entries = entries.astype(jnp.float32)
    return entries * lax.rsqrt(jnp.sum(entries * entries, axis=-1, keepdims=True) + 1e-06)


def lower_inverse(below_part):
    length = below_part.shape[-1]
    identity = jnp.eye(length, dtype=jnp.float32)
    result = identity - below_part
    raised = below_part
    doubled = 2
    while doubled < length:
        raised = jnp.einsum("nij,njk->nik", raised, raised, precision=highest)
        result = jnp.einsum("nij,njk->nik", result, identity + raised, precision=highest)
        doubled = doubled * 2
    return result


def prepare(queries, key_rows, values, rate_rows):
    n_groups = queries.shape[0] // GROUP_TOKENS
    q_unit = unit_rows(queries).reshape(n_groups, GROUP_TOKENS, -1)
    k_unit = unit_rows(key_rows).reshape(n_groups, GROUP_TOKENS, -1)
    val_units = values.astype(jnp.float32).reshape(n_groups, GROUP_TOKENS, -1)
    rate_col = rate_rows.reshape(n_groups, GROUP_TOKENS, 1)
    key_inner = jnp.einsum("nik,njk->nij", k_unit, k_unit, precision=highest)
    positions = jnp.arange(GROUP_TOKENS)
    is_below = positions[:, None] > positions[None, :]
    on_or_below = positions[:, None] >= positions[None, :]
    below_part = jnp.where(is_below[None], rate_col * key_inner, 0.0)
    inverse = lower_inverse(below_part)
    writes = jnp.einsum("nij,njk->nik", inverse, rate_col * k_unit, precision=highest)
    updates = jnp.einsum("nij,njk->nik", inverse, rate_col * val_units, precision=highest)
    query_key = jnp.where(
        on_or_below[None], jnp.einsum("nik,njk->nij", q_unit, k_unit, precision=highest), 0.0
    )
    return (q_unit, k_unit, writes, updates, query_key)


def local_pair(k_unit, writes, updates):
    head_size = k_unit.shape[-1]
    identity = jnp.eye(head_size, dtype=jnp.float32)

    def stride(carry, inputs_now):
        transit, carried = carry
        k_block, w_block, u_block = inputs_now
        stepped = identity - jnp.dot(k_block.T, w_block, precision=highest)
        transit = jnp.dot(stepped, transit, precision=highest)
        carried = jnp.dot(stepped, carried, precision=highest) + jnp.dot(
            k_block.T, u_block, precision=highest
        )
        return ((transit, carried), None)

    start_pair = (identity, jnp.zeros((head_size, head_size), jnp.float32))
    (transit, carried), _ = lax.scan(stride, start_pair, (k_unit, writes, updates))
    return (transit, carried)


def local_affine(q_unit, k_unit, writes, updates, query_key):
    n_blocks, _, head_size = k_unit.shape
    identity = jnp.eye(head_size, dtype=jnp.float32)
    key_cols = jnp.swapaxes(k_unit, -1, -2)
    stepped = identity - jnp.einsum("nij,njk->nik", key_cols, writes, precision=highest)
    written = jnp.einsum("nij,njk->nik", key_cols, updates, precision=highest)
    transit_list = [identity]
    carried_list = [jnp.zeros_like(identity)]
    for block in range(n_blocks):
        transit_list.append(jnp.dot(stepped[block], transit_list[-1], precision=highest))
        carried_list.append(
            jnp.dot(stepped[block], carried_list[-1], precision=highest) + written[block]
        )
    transit_before = jnp.stack(transit_list[:-1])
    carried_before = jnp.stack(carried_list[:-1])
    reading = q_unit - jnp.einsum("nij,njk->nik", query_key, writes, precision=highest)
    slope = jnp.einsum("nij,njk->nik", reading, transit_before, precision=highest)
    offset = jnp.einsum("nij,njk->nik", reading, carried_before, precision=highest) + jnp.einsum(
        "nij,njk->nik", query_key, updates, precision=highest
    )
    rows = n_blocks * k_unit.shape[1]
    return (
        transit_list[-1],
        carried_list[-1],
        slope.reshape(rows, head_size),
        offset.reshape(rows, head_size),
    )


def advance(carried, inputs_now):
    q_block, k_block, w_block, u_block, cross_block = inputs_now
    corrected = u_block - jnp.dot(w_block, carried, precision=highest)
    result_now = jnp.dot(q_block, carried, precision=highest) + jnp.dot(
        cross_block, corrected, precision=highest
    )
    return (carried + jnp.dot(k_block.T, corrected, precision=highest), result_now)


def run_blocks(carried_in, q_unit, k_unit, writes, updates, query_key):
    _, results = lax.scan(advance, carried_in, (q_unit, k_unit, writes, updates, query_key))
    return results


def batched_dot(left, right):
    return jnp.einsum("hij,hjk->hik", left, right, precision=highest)


def on_device(q_delta, k_delta, v_delta, write_rate, q_attn, k_attn, out_gain):
    tok_rows, features = q_delta.shape
    heads_here = write_rate.shape[1]
    head_size = features // heads_here

    def by_head(entries):
        return entries.reshape(tok_rows, heads_here, head_size).transpose(1, 0, 2)

    q_unit, k_unit, writes, updates, query_key = jax.vmap(prepare)(
        by_head(q_delta), by_head(k_delta), by_head(v_delta), write_rate.T
    )
    shard_reach = WINDOW // tok_rows

    def window_rows(own, lanes, opened=()):
        lane_length = -(-shard_reach // lanes)
        pieces = []
        for lane in range(lanes):
            first = lane * lane_length + 1
            last = min(shard_reach, (lane + 1) * lane_length)
            piece = opened[lane] if lane < len(opened) else shifted(own, "seq", first)
            pieces.append(piece)
            for _ in range(first, last):
                piece = shifted(piece, "seq", 1)
                pieces.append(piece)
        return jnp.concatenate(pieces[::-1] + [own], axis=0)

    transit, carried, slope, offset = jax.vmap(local_affine)(
        q_unit, k_unit, writes, updates, query_key
    )
    key_near = shifted(k_attn, "seq", 1)
    key_far = shifted(k_attn, "seq", -(-shard_reach // 2) + 1)
    transit, carried, key_far = lax.optimization_barrier((transit, carried, key_far))
    position = lax.axis_index("seq")
    seq_size = lax.axis_size("seq")
    group = min(4, seq_size)
    rank = position % group

    def moved(value, by, sources):
        pairs = [(i, i + by) for i in sources if 0 <= i + by < seq_size]
        return lax.ppermute(value, "seq", pairs)

    identity = jnp.broadcast_to(jnp.eye(head_size, dtype=jnp.float32), transit.shape)
    before_transit = identity
    before_carried = jnp.zeros_like(carried)
    distance = 1
    while distance < group:
        inside = [i for i in range(seq_size) if i % group + distance < group]
        transit_prev = moved(transit, distance, inside)
        carried_prev = moved(carried, distance, inside)
        has_prev = rank >= distance
        before_carried = jnp.where(
            has_prev, batched_dot(before_transit, carried_prev) + before_carried, before_carried
        )
        before_transit = jnp.where(has_prev, batched_dot(before_transit, transit_prev), before_transit)
        carried_in = jnp.where(has_prev, batched_dot(transit, carried_prev) + carried, carried)
        transit = jnp.where(has_prev, batched_dot(transit, transit_prev), transit)
        carried = carried_in
        distance *= 2
    ends = [i for i in range(seq_size) if i % group == group - 1]
    end_transit, end_carried = transit, carried
    distance = group
    while distance < seq_size:
        final = 2 * distance >= seq_size
        carried_prev = moved(end_carried, distance, ends)
        has_prev = (rank == group - 1) & (position >= distance)
        carried_next = jnp.where(
            has_prev, batched_dot(end_transit, carried_prev) + end_carried, end_carried
        )
        if not final:
            transit_prev = moved(end_transit, distance, ends)
            end_transit = jnp.where(has_prev, batched_dot(end_transit, transit_prev), end_transit)
        end_carried = carried_next
        distance *= 2
    group_in = jnp.zeros_like(carried)
    for hop in range(1, group + 1):
        group_in = group_in + moved(end_carried, hop, ends)
    offset = offset + batched_dot(slope, before_carried)
    slope = batched_dot(slope, before_transit)
    results = batched_dot(slope, group_in) + offset
    delta_out = (
        results.reshape(heads_here, tok_rows, head_size)
        .transpose(1, 0, 2)
        .reshape(tok_rows, features)
        .astype(jnp.bfloat16)
    )
    rows_all = (window_rows(k_attn, 2, (key_near, key_far)), window_rows(delta_out, 2))
    block_rows = min(512, tok_rows)
    first_row = lax.axis_index("seq") * tok_rows
    score_scale = 1.0 / math.sqrt(head_size)

    def attend_block(block_start):
        queries = q_attn.reshape(block_rows, heads_here, head_size)
        near_keys = rows_all[0].reshape(WINDOW + block_rows, heads_here, head_size)
        near_values = rows_all[1].reshape(WINDOW + block_rows, heads_here, head_size)
        scores = (
            jnp.einsum("qhd,khd->hqk", queries, near_keys, preferred_element_type=jnp.float32)
            * score_scale
        )
        q_index = jnp.arange(block_rows)[:, None]
        k_index = jnp.arange(WINDOW + block_rows)[None, :]
        allowed = (
            (k_index > q_index)
            & (k_index <= q_index + WINDOW)
            & (first_row + block_start + k_index >= WINDOW)
        )
        row_top = jnp.max(jnp.where(allowed[None], scores, -1e30), axis=2, keepdims=True)
        exps = jnp.exp(jnp.where(allowed[None], scores - row_top, -1e30))
        weights = (exps / jnp.sum(exps, axis=2, keepdims=True)).astype(jnp.bfloat16)
        mixed_rows = jnp.einsum(
            "hqk,khd->qhd", weights, near_values, preferred_element_type=jnp.float32
        )
        return mixed_rows.reshape(block_rows, features)

    starts = jnp.arange(tok_rows // block_rows) * block_rows
    attended = lax.map(attend_block, starts).reshape(tok_rows, features)
    squares = jnp.sum(attended * attended, axis=1)
    total_sq = lax.psum(squares, "head")
    scale_rows = lax.rsqrt(total_sq / (features * lax.axis_size("head")) + 1e-06)
    normed_out = (attended * out_gain[None, :] * scale_rows[:, None]).astype(jnp.bfloat16)
    return (delta_out, normed_out)


def solution(mesh):
    placed = (
        P("seq", "head"),
        P("seq", "head"),
        P("seq", "head"),
        P("seq", "head"),
        P("seq", "head"),
        P("seq", "head"),
        P("head"),
    )
    return jax.shard_map(
        on_device,
        mesh=mesh,
        in_specs=placed,
        out_specs=(P("seq", "head"), P("seq", "head")),
        check_vma=False,
    )
```

```python
import math

import jax
import jax.numpy as jnp
from jax import lax
from jax.sharding import Mesh, PartitionSpec as P

GROUP_TOKENS = 64
SEQ = ("rows", "cols")
WINDOW = 2048


highest = lax.Precision.HIGHEST


def shifted(value, axis, by):
    size = lax.axis_size(axis)
    pairs = [(i, i + by) for i in range(size) if 0 <= i + by < size]
    return lax.ppermute(value, axis, pairs)


def unit_rows(entries):
    entries = entries.astype(jnp.float32)
    return entries * lax.rsqrt(jnp.sum(entries * entries, axis=-1, keepdims=True) + 1e-06)


def lower_inverse(below_part):
    length = below_part.shape[-1]
    identity = jnp.eye(length, dtype=jnp.float32)
    result = identity - below_part
    raised = below_part
    doubled = 2
    while doubled < length:
        raised = jnp.einsum("nij,njk->nik", raised, raised, precision=highest)
        result = jnp.einsum("nij,njk->nik", result, identity + raised, precision=highest)
        doubled = doubled * 2
    return result


def prepare(queries, key_rows, values, rate_rows):
    n_groups = queries.shape[0] // GROUP_TOKENS
    q_unit = unit_rows(queries).reshape(n_groups, GROUP_TOKENS, -1)
    k_unit = unit_rows(key_rows).reshape(n_groups, GROUP_TOKENS, -1)
    val_units = values.astype(jnp.float32).reshape(n_groups, GROUP_TOKENS, -1)
    rate_col = rate_rows.reshape(n_groups, GROUP_TOKENS, 1)
    key_inner = jnp.einsum("nik,njk->nij", k_unit, k_unit, precision=highest)
    positions = jnp.arange(GROUP_TOKENS)
    is_below = positions[:, None] > positions[None, :]
    on_or_below = positions[:, None] >= positions[None, :]
    below_part = jnp.where(is_below[None], rate_col * key_inner, 0.0)
    inverse = lower_inverse(below_part)
    writes = jnp.einsum("nij,njk->nik", inverse, rate_col * k_unit, precision=highest)
    updates = jnp.einsum("nij,njk->nik", inverse, rate_col * val_units, precision=highest)
    query_key = jnp.where(
        on_or_below[None], jnp.einsum("nik,njk->nij", q_unit, k_unit, precision=highest), 0.0
    )
    return (q_unit, k_unit, writes, updates, query_key)


def local_pair(k_unit, writes, updates):
    head_size = k_unit.shape[-1]
    identity = jnp.eye(head_size, dtype=jnp.float32)

    def stride(carry, inputs_now):
        transit, carried = carry
        k_block, w_block, u_block = inputs_now
        stepped = identity - jnp.dot(k_block.T, w_block, precision=highest)
        transit = jnp.dot(stepped, transit, precision=highest)
        carried = jnp.dot(stepped, carried, precision=highest) + jnp.dot(
            k_block.T, u_block, precision=highest
        )
        return ((transit, carried), None)

    start_pair = (identity, jnp.zeros((head_size, head_size), jnp.float32))
    (transit, carried), _ = lax.scan(stride, start_pair, (k_unit, writes, updates))
    return (transit, carried)


def advance(carried, inputs_now):
    q_block, k_block, w_block, u_block, cross_block = inputs_now
    corrected = u_block - jnp.dot(w_block, carried, precision=highest)
    result_now = jnp.dot(q_block, carried, precision=highest) + jnp.dot(
        cross_block, corrected, precision=highest
    )
    return (carried + jnp.dot(k_block.T, corrected, precision=highest), result_now)


def run_blocks(carried_in, q_unit, k_unit, writes, updates, query_key):
    _, results = lax.scan(advance, carried_in, (q_unit, k_unit, writes, updates, query_key))
    return results


def batched_dot(left, right):
    return jnp.einsum("hij,hjk->hik", left, right, precision=highest)


def on_device(q_delta, k_delta, v_delta, write_rate, q_attn, k_attn, out_gain):
    tok_rows, features = q_delta.shape
    heads_here = write_rate.shape[1]
    head_size = features // heads_here

    def by_head(entries):
        return entries.reshape(tok_rows, heads_here, head_size).transpose(1, 0, 2)

    q_unit, k_unit, writes, updates, query_key = jax.vmap(prepare)(
        by_head(q_delta), by_head(k_delta), by_head(v_delta), write_rate.T
    )
    transit, carried = jax.vmap(local_pair)(k_unit, writes, updates)
    position = lax.axis_index(SEQ)
    seq_size = lax.axis_size(SEQ)
    group = min(4, seq_size)
    rank = position % group

    def moved(value, by, sources):
        pairs = [(i, i + by) for i in sources if 0 <= i + by < seq_size]
        return lax.ppermute(value, SEQ, pairs)

    identity = jnp.broadcast_to(jnp.eye(head_size, dtype=jnp.float32), transit.shape)
    before_transit = identity
    before_carried = jnp.zeros_like(carried)
    distance = 1
    while distance < group:
        inside = [i for i in range(seq_size) if i % group + distance < group]
        transit_prev = moved(transit, distance, inside)
        carried_prev = moved(carried, distance, inside)
        has_prev = rank >= distance
        before_carried = jnp.where(
            has_prev, batched_dot(before_transit, carried_prev) + before_carried, before_carried
        )
        before_transit = jnp.where(has_prev, batched_dot(before_transit, transit_prev), before_transit)
        carried_in = jnp.where(has_prev, batched_dot(transit, carried_prev) + carried, carried)
        transit = jnp.where(has_prev, batched_dot(transit, transit_prev), transit)
        carried = carried_in
        distance *= 2
    ends = [i for i in range(seq_size) if i % group == group - 1]
    end_transit, end_carried = transit, carried
    distance = group
    while distance < seq_size:
        final = 2 * distance >= seq_size
        carried_prev = moved(end_carried, distance, ends)
        has_prev = (rank == group - 1) & (position >= distance)
        carried_next = jnp.where(
            has_prev, batched_dot(end_transit, carried_prev) + end_carried, end_carried
        )
        if not final:
            transit_prev = moved(end_transit, distance, ends)
            end_transit = jnp.where(has_prev, batched_dot(end_transit, transit_prev), end_transit)
        end_carried = carried_next
        distance *= 2
    group_in = jnp.zeros_like(carried)
    for hop in range(1, group + 1):
        group_in = group_in + moved(end_carried, hop, ends)
    incoming = batched_dot(before_transit, group_in) + before_carried
    results = jax.vmap(run_blocks)(incoming, q_unit, k_unit, writes, updates, query_key)
    delta_out = (
        results.reshape(heads_here, tok_rows, head_size)
        .transpose(1, 0, 2)
        .reshape(tok_rows, features)
        .astype(jnp.bfloat16)
    )
    shard_reach = WINDOW // tok_rows

    def window_rows(own, lanes):
        lane_length = -(-shard_reach // lanes)
        pieces = []
        for lane in range(lanes):
            first = lane * lane_length + 1
            last = min(shard_reach, (lane + 1) * lane_length)
            piece = shifted(own, SEQ, first)
            pieces.append(piece)
            for _ in range(first, last):
                piece = shifted(piece, SEQ, 1)
                pieces.append(piece)
        return jnp.concatenate(pieces[::-1] + [own], axis=0)

    row_count = lax.axis_size("rows")
    col_count = lax.axis_size("cols")
    prev_row = lax.ppermute(k_attn, "rows", [(i, i + 1) for i in range(row_count - 1)])
    gathered = lax.all_gather(jnp.stack((prev_row, k_attn)), "cols")
    flat = jnp.concatenate((gathered[:, 0], gathered[:, 1]), axis=0)
    near = lax.dynamic_slice_in_dim(
        flat, lax.axis_index("cols") + col_count - shard_reach, shard_reach, 0
    )
    key_rows = jnp.concatenate((near.reshape(shard_reach * tok_rows, features), k_attn), axis=0)
    rows_all = (key_rows, window_rows(delta_out, 2))
    block_rows = min(512, tok_rows)
    first_row = lax.axis_index(SEQ) * tok_rows
    score_scale = 1.0 / math.sqrt(head_size)

    def attend_block(block_start):
        queries = q_attn.reshape(block_rows, heads_here, head_size)
        near_keys = rows_all[0].reshape(WINDOW + block_rows, heads_here, head_size)
        near_values = rows_all[1].reshape(WINDOW + block_rows, heads_here, head_size)
        scores = (
            jnp.einsum("qhd,khd->hqk", queries, near_keys, preferred_element_type=jnp.float32)
            * score_scale
        )
        q_index = jnp.arange(block_rows)[:, None]
        k_index = jnp.arange(WINDOW + block_rows)[None, :]
        allowed = (
            (k_index > q_index)
            & (k_index <= q_index + WINDOW)
            & (first_row + block_start + k_index >= WINDOW)
        )
        row_top = jnp.max(jnp.where(allowed[None], scores, -1e30), axis=2, keepdims=True)
        exps = jnp.exp(jnp.where(allowed[None], scores - row_top, -1e30))
        weights = (exps / jnp.sum(exps, axis=2, keepdims=True)).astype(jnp.bfloat16)
        mixed_rows = jnp.einsum(
            "hqk,khd->qhd", weights, near_values, preferred_element_type=jnp.float32
        )
        return mixed_rows.reshape(block_rows, features)

    starts = jnp.arange(tok_rows // block_rows) * block_rows
    attended = lax.map(attend_block, starts).reshape(tok_rows, features)
    squares = jnp.sum(attended * attended, axis=1)
    total_sq = lax.psum(squares, "head")
    scale_rows = lax.rsqrt(total_sq / (features * lax.axis_size("head")) + 1e-06)
    normed_out = (attended * out_gain[None, :] * scale_rows[:, None]).astype(jnp.bfloat16)
    return (delta_out, normed_out)


def solution(mesh):
    seq_devices = mesh.devices[:, 0]
    cols = len({device.coords[-1] for device in seq_devices})
    row_mesh = Mesh(
        mesh.devices.reshape(mesh.shape["seq"] // cols, cols, mesh.shape["head"]),
        ("rows", "cols", "head"),
    )
    placed = (
        P(SEQ, "head"),
        P(SEQ, "head"),
        P(SEQ, "head"),
        P(SEQ, "head"),
        P(SEQ, "head"),
        P(SEQ, "head"),
        P("head"),
    )
    return jax.shard_map(
        on_device,
        mesh=row_mesh,
        in_specs=placed,
        out_specs=(P(SEQ, "head"), P(SEQ, "head")),
        check_vma=False,
    )
```

```python
import math

import jax
import jax.numpy as jnp
from jax import lax
from jax.sharding import PartitionSpec as P

GROUP_TOKENS = 64
WINDOW = 2048


highest = lax.Precision.HIGHEST


def shifted(value, axis, by):
    size = lax.axis_size(axis)
    pairs = [(i, i + by) for i in range(size) if 0 <= i + by < size]
    return lax.ppermute(value, axis, pairs)


def unit_rows(entries):
    entries = entries.astype(jnp.float32)
    return entries * lax.rsqrt(jnp.sum(entries * entries, axis=-1, keepdims=True) + 1e-06)


def lower_inverse(below_part):
    length = below_part.shape[-1]
    identity = jnp.eye(length, dtype=jnp.float32)
    result = identity - below_part
    raised = below_part
    doubled = 2
    while doubled < length:
        raised = jnp.einsum("nij,njk->nik", raised, raised, precision=highest)
        result = jnp.einsum("nij,njk->nik", result, identity + raised, precision=highest)
        doubled = doubled * 2
    return result


def prepare(queries, key_rows, values, rate_rows):
    n_groups = queries.shape[0] // GROUP_TOKENS
    q_unit = unit_rows(queries).reshape(n_groups, GROUP_TOKENS, -1)
    k_unit = unit_rows(key_rows).reshape(n_groups, GROUP_TOKENS, -1)
    val_units = values.astype(jnp.float32).reshape(n_groups, GROUP_TOKENS, -1)
    rate_col = rate_rows.reshape(n_groups, GROUP_TOKENS, 1)
    key_inner = jnp.einsum("nik,njk->nij", k_unit, k_unit, precision=highest)
    positions = jnp.arange(GROUP_TOKENS)
    is_below = positions[:, None] > positions[None, :]
    on_or_below = positions[:, None] >= positions[None, :]
    below_part = jnp.where(is_below[None], rate_col * key_inner, 0.0)
    inverse = lower_inverse(below_part)
    writes = jnp.einsum("nij,njk->nik", inverse, rate_col * k_unit, precision=highest)
    updates = jnp.einsum("nij,njk->nik", inverse, rate_col * val_units, precision=highest)
    query_key = jnp.where(
        on_or_below[None], jnp.einsum("nik,njk->nij", q_unit, k_unit, precision=highest), 0.0
    )
    return (q_unit, k_unit, writes, updates, query_key)


def local_pair(k_unit, writes, updates):
    head_size = k_unit.shape[-1]
    identity = jnp.eye(head_size, dtype=jnp.float32)

    def stride(carry, inputs_now):
        transit, carried = carry
        k_block, w_block, u_block = inputs_now
        stepped = identity - jnp.dot(k_block.T, w_block, precision=highest)
        transit = jnp.dot(stepped, transit, precision=highest)
        carried = jnp.dot(stepped, carried, precision=highest) + jnp.dot(
            k_block.T, u_block, precision=highest
        )
        return ((transit, carried), None)

    start_pair = (identity, jnp.zeros((head_size, head_size), jnp.float32))
    (transit, carried), _ = lax.scan(stride, start_pair, (k_unit, writes, updates))
    return (transit, carried)


def advance(carried, inputs_now):
    q_block, k_block, w_block, u_block, cross_block = inputs_now
    corrected = u_block - jnp.dot(w_block, carried, precision=highest)
    result_now = jnp.dot(q_block, carried, precision=highest) + jnp.dot(
        cross_block, corrected, precision=highest
    )
    return (carried + jnp.dot(k_block.T, corrected, precision=highest), result_now)


def run_blocks(carried_in, q_unit, k_unit, writes, updates, query_key):
    _, results = lax.scan(advance, carried_in, (q_unit, k_unit, writes, updates, query_key))
    return results


def batched_dot(left, right):
    return jnp.einsum("hij,hjk->hik", left, right, precision=highest)


def on_device(q_delta, k_delta, v_delta, write_rate, q_attn, k_attn, out_gain):
    tok_rows, features = q_delta.shape
    heads_here = write_rate.shape[1]
    head_size = features // heads_here

    def by_head(entries):
        return entries.reshape(tok_rows, heads_here, head_size).transpose(1, 0, 2)

    q_unit, k_unit, writes, updates, query_key = jax.vmap(prepare)(
        by_head(q_delta), by_head(k_delta), by_head(v_delta), write_rate.T
    )
    transit, carried = jax.vmap(local_pair)(k_unit, writes, updates)
    position = lax.axis_index("seq")
    seq_size = lax.axis_size("seq")
    group = min(2, seq_size)
    rank = position % group

    def moved(value, by, sources):
        pairs = [(i, i + by) for i in sources if 0 <= i + by < seq_size]
        return lax.ppermute(value, "seq", pairs)

    identity = jnp.broadcast_to(jnp.eye(head_size, dtype=jnp.float32), transit.shape)
    before_transit = identity
    before_carried = jnp.zeros_like(carried)
    distance = 1
    while distance < group:
        inside = [i for i in range(seq_size) if i % group + distance < group]
        transit_prev = moved(transit, distance, inside)
        carried_prev = moved(carried, distance, inside)
        has_prev = rank >= distance
        before_carried = jnp.where(
            has_prev, batched_dot(before_transit, carried_prev) + before_carried, before_carried
        )
        before_transit = jnp.where(has_prev, batched_dot(before_transit, transit_prev), before_transit)
        carried_in = jnp.where(has_prev, batched_dot(transit, carried_prev) + carried, carried)
        transit = jnp.where(has_prev, batched_dot(transit, transit_prev), transit)
        carried = carried_in
        distance *= 2
    ends = [i for i in range(seq_size) if i % group == group - 1]
    end_transit, end_carried = transit, carried
    distance = group
    while distance < seq_size:
        final = 2 * distance >= seq_size
        carried_prev = moved(end_carried, distance, ends)
        has_prev = (rank == group - 1) & (position >= distance)
        carried_next = jnp.where(
            has_prev, batched_dot(end_transit, carried_prev) + end_carried, end_carried
        )
        if not final:
            transit_prev = moved(end_transit, distance, ends)
            end_transit = jnp.where(has_prev, batched_dot(end_transit, transit_prev), end_transit)
        end_carried = carried_next
        distance *= 2
    group_in = jnp.zeros_like(carried)
    for hop in range(1, group + 1):
        group_in = group_in + moved(end_carried, hop, ends)
    incoming = batched_dot(before_transit, group_in) + before_carried
    results = jax.vmap(run_blocks)(incoming, q_unit, k_unit, writes, updates, query_key)
    delta_out = (
        results.reshape(heads_here, tok_rows, head_size)
        .transpose(1, 0, 2)
        .reshape(tok_rows, features)
        .astype(jnp.bfloat16)
    )
    shard_reach = WINDOW // tok_rows

    def window_rows(own, lanes):
        lane_length = -(-shard_reach // lanes)
        pieces = []
        for lane in range(lanes):
            first = lane * lane_length + 1
            last = min(shard_reach, (lane + 1) * lane_length)
            piece = shifted(own, "seq", first)
            pieces.append(piece)
            for _ in range(first, last):
                piece = shifted(piece, "seq", 1)
                pieces.append(piece)
        return jnp.concatenate(pieces[::-1] + [own], axis=0)

    rows_all = (window_rows(k_attn, 1), window_rows(delta_out, 2))
    block_rows = min(512, tok_rows)
    first_row = lax.axis_index("seq") * tok_rows
    score_scale = 1.0 / math.sqrt(head_size)

    def attend_block(block_start):
        queries = q_attn.reshape(block_rows, heads_here, head_size)
        near_keys = rows_all[0].reshape(WINDOW + block_rows, heads_here, head_size)
        near_values = rows_all[1].reshape(WINDOW + block_rows, heads_here, head_size)
        scores = (
            jnp.einsum("qhd,khd->hqk", queries, near_keys, preferred_element_type=jnp.float32)
            * score_scale
        )
        q_index = jnp.arange(block_rows)[:, None]
        k_index = jnp.arange(WINDOW + block_rows)[None, :]
        allowed = (
            (k_index > q_index)
            & (k_index <= q_index + WINDOW)
            & (first_row + block_start + k_index >= WINDOW)
        )
        row_top = jnp.max(jnp.where(allowed[None], scores, -1e30), axis=2, keepdims=True)
        exps = jnp.exp(jnp.where(allowed[None], scores - row_top, -1e30))
        weights = (exps / jnp.sum(exps, axis=2, keepdims=True)).astype(jnp.bfloat16)
        mixed_rows = jnp.einsum(
            "hqk,khd->qhd", weights, near_values, preferred_element_type=jnp.float32
        )
        return mixed_rows.reshape(block_rows, features)

    starts = jnp.arange(tok_rows // block_rows) * block_rows
    attended = lax.map(attend_block, starts).reshape(tok_rows, features)
    squares = jnp.sum(attended * attended, axis=1)
    total_sq = lax.psum(squares, "head")
    scale_rows = lax.rsqrt(total_sq / (features * lax.axis_size("head")) + 1e-06)
    normed_out = (attended * out_gain[None, :] * scale_rows[:, None]).astype(jnp.bfloat16)
    return (delta_out, normed_out)


def solution(mesh):
    placed = (
        P("seq", "head"),
        P("seq", "head"),
        P("seq", "head"),
        P("seq", "head"),
        P("seq", "head"),
        P("seq", "head"),
        P("head"),
    )
    return jax.shard_map(
        on_device,
        mesh=mesh,
        in_specs=placed,
        out_specs=(P("seq", "head"), P("seq", "head")),
        check_vma=False,
    )
```

```python
import math

import jax
import jax.numpy as jnp
from jax import lax
from jax.sharding import PartitionSpec as P

GROUP_TOKENS = 64
WINDOW = 2048


highest = lax.Precision.HIGHEST


def shifted(value, axis, by):
    size = lax.axis_size(axis)
    pairs = [(i, i + by) for i in range(size) if 0 <= i + by < size]
    return lax.ppermute(value, axis, pairs)


def unit_rows(entries):
    entries = entries.astype(jnp.float32)
    return entries * lax.rsqrt(jnp.sum(entries * entries, axis=-1, keepdims=True) + 1e-06)


def lower_inverse(below_part):
    length = below_part.shape[-1]
    identity = jnp.eye(length, dtype=jnp.float32)
    result = identity - below_part
    raised = below_part
    doubled = 2
    while doubled < length:
        raised = jnp.einsum("nij,njk->nik", raised, raised, precision=highest)
        result = jnp.einsum("nij,njk->nik", result, identity + raised, precision=highest)
        doubled = doubled * 2
    return result


def prepare(queries, key_rows, values, rate_rows):
    n_groups = queries.shape[0] // GROUP_TOKENS
    q_unit = unit_rows(queries).reshape(n_groups, GROUP_TOKENS, -1)
    k_unit = unit_rows(key_rows).reshape(n_groups, GROUP_TOKENS, -1)
    val_units = values.astype(jnp.float32).reshape(n_groups, GROUP_TOKENS, -1)
    rate_col = rate_rows.reshape(n_groups, GROUP_TOKENS, 1)
    key_inner = jnp.einsum("nik,njk->nij", k_unit, k_unit, precision=highest)
    positions = jnp.arange(GROUP_TOKENS)
    is_below = positions[:, None] > positions[None, :]
    on_or_below = positions[:, None] >= positions[None, :]
    below_part = jnp.where(is_below[None], rate_col * key_inner, 0.0)
    inverse = lower_inverse(below_part)
    writes = jnp.einsum("nij,njk->nik", inverse, rate_col * k_unit, precision=highest)
    updates = jnp.einsum("nij,njk->nik", inverse, rate_col * val_units, precision=highest)
    query_key = jnp.where(
        on_or_below[None], jnp.einsum("nik,njk->nij", q_unit, k_unit, precision=highest), 0.0
    )
    return (q_unit, k_unit, writes, updates, query_key)


def local_pair(k_unit, writes, updates):
    head_size = k_unit.shape[-1]
    identity = jnp.eye(head_size, dtype=jnp.float32)

    def stride(carry, inputs_now):
        transit, carried = carry
        k_block, w_block, u_block = inputs_now
        stepped = identity - jnp.dot(k_block.T, w_block, precision=highest)
        transit = jnp.dot(stepped, transit, precision=highest)
        carried = jnp.dot(stepped, carried, precision=highest) + jnp.dot(
            k_block.T, u_block, precision=highest
        )
        return ((transit, carried), None)

    start_pair = (identity, jnp.zeros((head_size, head_size), jnp.float32))
    (transit, carried), _ = lax.scan(stride, start_pair, (k_unit, writes, updates))
    return (transit, carried)


def advance(carried, inputs_now):
    q_block, k_block, w_block, u_block, cross_block = inputs_now
    corrected = u_block - jnp.dot(w_block, carried, precision=highest)
    result_now = jnp.dot(q_block, carried, precision=highest) + jnp.dot(
        cross_block, corrected, precision=highest
    )
    return (carried + jnp.dot(k_block.T, corrected, precision=highest), result_now)


def run_blocks(carried_in, q_unit, k_unit, writes, updates, query_key):
    _, results = lax.scan(advance, carried_in, (q_unit, k_unit, writes, updates, query_key))
    return results


def batched_dot(left, right):
    return jnp.einsum("hij,hjk->hik", left, right, precision=highest)


def on_device(q_delta, k_delta, v_delta, write_rate, q_attn, k_attn, out_gain):
    tok_rows, features = q_delta.shape
    heads_here = write_rate.shape[1]
    head_size = features // heads_here

    def by_head(entries):
        return entries.reshape(tok_rows, heads_here, head_size).transpose(1, 0, 2)

    q_unit, k_unit, writes, updates, query_key = jax.vmap(prepare)(
        by_head(q_delta), by_head(k_delta), by_head(v_delta), write_rate.T
    )
    transit, carried = jax.vmap(local_pair)(k_unit, writes, updates)
    position = lax.axis_index("seq")
    seq_size = lax.axis_size("seq")
    group = min(4, seq_size)
    rank = position % group

    def moved(value, by, sources):
        pairs = [(i, i + by) for i in sources if 0 <= i + by < seq_size]
        return lax.ppermute(value, "seq", pairs)

    identity = jnp.broadcast_to(jnp.eye(head_size, dtype=jnp.float32), transit.shape)
    before_transit = identity
    before_carried = jnp.zeros_like(carried)
    distance = 1
    while distance < group:
        inside = [i for i in range(seq_size) if i % group + distance < group]
        transit_prev = moved(transit, distance, inside)
        carried_prev = moved(carried, distance, inside)
        has_prev = rank >= distance
        before_carried = jnp.where(
            has_prev, batched_dot(before_transit, carried_prev) + before_carried, before_carried
        )
        before_transit = jnp.where(has_prev, batched_dot(before_transit, transit_prev), before_transit)
        carried_in = jnp.where(has_prev, batched_dot(transit, carried_prev) + carried, carried)
        transit = jnp.where(has_prev, batched_dot(transit, transit_prev), transit)
        carried = carried_in
        distance *= 2
    ends = [i for i in range(seq_size) if i % group == group - 1]
    end_transit, end_carried = transit, carried
    distance = group
    while distance < seq_size:
        final = 2 * distance >= seq_size
        carried_prev = moved(end_carried, distance, ends)
        has_prev = (rank == group - 1) & (position >= distance)
        carried_next = jnp.where(
            has_prev, batched_dot(end_transit, carried_prev) + end_carried, end_carried
        )
        if not final:
            transit_prev = moved(end_transit, distance, ends)
            end_transit = jnp.where(has_prev, batched_dot(end_transit, transit_prev), end_transit)
        end_carried = carried_next
        distance *= 2
    group_in = jnp.zeros_like(carried)
    for hop in range(1, group + 1):
        group_in = group_in + moved(end_carried, hop, ends)
    incoming = batched_dot(before_transit, group_in) + before_carried
    results = jax.vmap(run_blocks)(incoming, q_unit, k_unit, writes, updates, query_key)
    delta_out = (
        results.reshape(heads_here, tok_rows, head_size)
        .transpose(1, 0, 2)
        .reshape(tok_rows, features)
        .astype(jnp.bfloat16)
    )
    shard_reach = WINDOW // tok_rows

    def window_rows(own, lanes):
        lane_length = -(-shard_reach // lanes)
        pieces = []
        for lane in range(lanes):
            first = lane * lane_length + 1
            last = min(shard_reach, (lane + 1) * lane_length)
            piece = shifted(own, "seq", first)
            pieces.append(piece)
            for _ in range(first, last):
                piece = shifted(piece, "seq", 1)
                pieces.append(piece)
        return jnp.concatenate(pieces[::-1] + [own], axis=0)

    rows_all = (window_rows(k_attn, 1), window_rows(delta_out, 3))
    block_rows = min(512, tok_rows)
    first_row = lax.axis_index("seq") * tok_rows
    score_scale = 1.0 / math.sqrt(head_size)

    def attend_block(block_start):
        queries = q_attn.reshape(block_rows, heads_here, head_size)
        near_keys = rows_all[0].reshape(WINDOW + block_rows, heads_here, head_size)
        near_values = rows_all[1].reshape(WINDOW + block_rows, heads_here, head_size)
        scores = (
            jnp.einsum("qhd,khd->hqk", queries, near_keys, preferred_element_type=jnp.float32)
            * score_scale
        )
        q_index = jnp.arange(block_rows)[:, None]
        k_index = jnp.arange(WINDOW + block_rows)[None, :]
        allowed = (
            (k_index > q_index)
            & (k_index <= q_index + WINDOW)
            & (first_row + block_start + k_index >= WINDOW)
        )
        row_top = jnp.max(jnp.where(allowed[None], scores, -1e30), axis=2, keepdims=True)
        exps = jnp.exp(jnp.where(allowed[None], scores - row_top, -1e30))
        weights = (exps / jnp.sum(exps, axis=2, keepdims=True)).astype(jnp.bfloat16)
        mixed_rows = jnp.einsum(
            "hqk,khd->qhd", weights, near_values, preferred_element_type=jnp.float32
        )
        return mixed_rows.reshape(block_rows, features)

    starts = jnp.arange(tok_rows // block_rows) * block_rows
    attended = lax.map(attend_block, starts).reshape(tok_rows, features)
    squares = jnp.sum(attended * attended, axis=1)
    total_sq = lax.psum(squares, "head")
    scale_rows = lax.rsqrt(total_sq / (features * lax.axis_size("head")) + 1e-06)
    normed_out = (attended * out_gain[None, :] * scale_rows[:, None]).astype(jnp.bfloat16)
    return (delta_out, normed_out)


def solution(mesh):
    placed = (
        P("seq", "head"),
        P("seq", "head"),
        P("seq", "head"),
        P("seq", "head"),
        P("seq", "head"),
        P("seq", "head"),
        P("head"),
    )
    return jax.shard_map(
        on_device,
        mesh=mesh,
        in_specs=placed,
        out_specs=(P("seq", "head"), P("seq", "head")),
        check_vma=False,
    )
```

```python
import math

import jax
import jax.numpy as jnp
from jax import lax
from jax.sharding import PartitionSpec as P

GROUP_TOKENS = 64
WINDOW = 2048


highest = lax.Precision.HIGHEST


def shifted(value, axis, by):
    size = lax.axis_size(axis)
    pairs = [(i, i + by) for i in range(size) if 0 <= i + by < size]
    return lax.ppermute(value, axis, pairs)


def unit_rows(entries):
    entries = entries.astype(jnp.float32)
    return entries * lax.rsqrt(jnp.sum(entries * entries, axis=-1, keepdims=True) + 1e-06)


def lower_inverse(below_part):
    length = below_part.shape[-1]
    identity = jnp.eye(length, dtype=jnp.float32)
    result = identity - below_part
    raised = below_part
    doubled = 2
    while doubled < length:
        raised = jnp.einsum("nij,njk->nik", raised, raised, precision=highest)
        result = jnp.einsum("nij,njk->nik", result, identity + raised, precision=highest)
        doubled = doubled * 2
    return result


def prepare(queries, key_rows, values, rate_rows):
    n_groups = queries.shape[0] // GROUP_TOKENS
    q_unit = unit_rows(queries).reshape(n_groups, GROUP_TOKENS, -1)
    k_unit = unit_rows(key_rows).reshape(n_groups, GROUP_TOKENS, -1)
    val_units = values.astype(jnp.float32).reshape(n_groups, GROUP_TOKENS, -1)
    rate_col = rate_rows.reshape(n_groups, GROUP_TOKENS, 1)
    key_inner = jnp.einsum("nik,njk->nij", k_unit, k_unit, precision=highest)
    positions = jnp.arange(GROUP_TOKENS)
    is_below = positions[:, None] > positions[None, :]
    on_or_below = positions[:, None] >= positions[None, :]
    below_part = jnp.where(is_below[None], rate_col * key_inner, 0.0)
    inverse = lower_inverse(below_part)
    writes = jnp.einsum("nij,njk->nik", inverse, rate_col * k_unit, precision=highest)
    updates = jnp.einsum("nij,njk->nik", inverse, rate_col * val_units, precision=highest)
    query_key = jnp.where(
        on_or_below[None], jnp.einsum("nik,njk->nij", q_unit, k_unit, precision=highest), 0.0
    )
    return (q_unit, k_unit, writes, updates, query_key)


def local_pair(k_unit, writes, updates):
    head_size = k_unit.shape[-1]
    identity = jnp.eye(head_size, dtype=jnp.float32)

    def stride(carry, inputs_now):
        transit, carried = carry
        k_block, w_block, u_block = inputs_now
        stepped = identity - jnp.dot(k_block.T, w_block, precision=highest)
        transit = jnp.dot(stepped, transit, precision=highest)
        carried = jnp.dot(stepped, carried, precision=highest) + jnp.dot(
            k_block.T, u_block, precision=highest
        )
        return ((transit, carried), None)

    start_pair = (identity, jnp.zeros((head_size, head_size), jnp.float32))
    (transit, carried), _ = lax.scan(stride, start_pair, (k_unit, writes, updates))
    return (transit, carried)


def advance(carried, inputs_now):
    q_block, k_block, w_block, u_block, cross_block = inputs_now
    corrected = u_block - jnp.dot(w_block, carried, precision=highest)
    result_now = jnp.dot(q_block, carried, precision=highest) + jnp.dot(
        cross_block, corrected, precision=highest
    )
    return (carried + jnp.dot(k_block.T, corrected, precision=highest), result_now)


def run_blocks(carried_in, q_unit, k_unit, writes, updates, query_key):
    _, results = lax.scan(advance, carried_in, (q_unit, k_unit, writes, updates, query_key))
    return results


def batched_dot(left, right):
    return jnp.einsum("hij,hjk->hik", left, right, precision=lax.Precision.HIGH)


def on_device(q_delta, k_delta, v_delta, write_rate, q_attn, k_attn, out_gain):
    tok_rows, features = q_delta.shape
    heads_here = write_rate.shape[1]
    head_size = features // heads_here

    def by_head(entries):
        return entries.reshape(tok_rows, heads_here, head_size).transpose(1, 0, 2)

    q_unit, k_unit, writes, updates, query_key = jax.vmap(prepare)(
        by_head(q_delta), by_head(k_delta), by_head(v_delta), write_rate.T
    )
    transit, carried = jax.vmap(local_pair)(k_unit, writes, updates)
    position = lax.axis_index("seq")
    seq_size = lax.axis_size("seq")
    group = min(4, seq_size)
    rank = position % group

    def moved(value, by, sources):
        pairs = [(i, i + by) for i in sources if 0 <= i + by < seq_size]
        return lax.ppermute(value, "seq", pairs)

    identity = jnp.broadcast_to(jnp.eye(head_size, dtype=jnp.float32), transit.shape)
    before_transit = identity
    before_carried = jnp.zeros_like(carried)
    distance = 1
    while distance < group:
        inside = [i for i in range(seq_size) if i % group + distance < group]
        transit_prev = moved(transit, distance, inside)
        carried_prev = moved(carried, distance, inside)
        has_prev = rank >= distance
        before_carried = jnp.where(
            has_prev, batched_dot(before_transit, carried_prev) + before_carried, before_carried
        )
        before_transit = jnp.where(has_prev, batched_dot(before_transit, transit_prev), before_transit)
        carried_in = jnp.where(has_prev, batched_dot(transit, carried_prev) + carried, carried)
        transit = jnp.where(has_prev, batched_dot(transit, transit_prev), transit)
        carried = carried_in
        distance *= 2
    ends = [i for i in range(seq_size) if i % group == group - 1]
    end_transit, end_carried = transit, carried
    distance = group
    while distance < seq_size:
        final = 2 * distance >= seq_size
        carried_prev = moved(end_carried, distance, ends)
        has_prev = (rank == group - 1) & (position >= distance)
        carried_next = jnp.where(
            has_prev, batched_dot(end_transit, carried_prev) + end_carried, end_carried
        )
        if not final:
            transit_prev = moved(end_transit, distance, ends)
            end_transit = jnp.where(has_prev, batched_dot(end_transit, transit_prev), end_transit)
        end_carried = carried_next
        distance *= 2
    group_in = jnp.zeros_like(carried)
    for hop in range(1, group + 1):
        group_in = group_in + moved(end_carried, hop, ends)
    incoming = batched_dot(before_transit, group_in) + before_carried
    results = jax.vmap(run_blocks)(incoming, q_unit, k_unit, writes, updates, query_key)
    delta_out = (
        results.reshape(heads_here, tok_rows, head_size)
        .transpose(1, 0, 2)
        .reshape(tok_rows, features)
        .astype(jnp.bfloat16)
    )
    shard_reach = WINDOW // tok_rows

    def window_rows(own, lanes):
        lane_length = -(-shard_reach // lanes)
        pieces = []
        for lane in range(lanes):
            first = lane * lane_length + 1
            last = min(shard_reach, (lane + 1) * lane_length)
            piece = shifted(own, "seq", first)
            pieces.append(piece)
            for _ in range(first, last):
                piece = shifted(piece, "seq", 1)
                pieces.append(piece)
        return jnp.concatenate(pieces[::-1] + [own], axis=0)

    rows_all = (window_rows(k_attn, 1), window_rows(delta_out, 2))
    block_rows = min(512, tok_rows)
    first_row = lax.axis_index("seq") * tok_rows
    score_scale = 1.0 / math.sqrt(head_size)

    def attend_block(block_start):
        queries = q_attn.reshape(block_rows, heads_here, head_size)
        near_keys = rows_all[0].reshape(WINDOW + block_rows, heads_here, head_size)
        near_values = rows_all[1].reshape(WINDOW + block_rows, heads_here, head_size)
        scores = (
            jnp.einsum("qhd,khd->hqk", queries, near_keys, preferred_element_type=jnp.float32)
            * score_scale
        )
        q_index = jnp.arange(block_rows)[:, None]
        k_index = jnp.arange(WINDOW + block_rows)[None, :]
        allowed = (
            (k_index > q_index)
            & (k_index <= q_index + WINDOW)
            & (first_row + block_start + k_index >= WINDOW)
        )
        row_top = jnp.max(jnp.where(allowed[None], scores, -1e30), axis=2, keepdims=True)
        exps = jnp.exp(jnp.where(allowed[None], scores - row_top, -1e30))
        weights = (exps / jnp.sum(exps, axis=2, keepdims=True)).astype(jnp.bfloat16)
        mixed_rows = jnp.einsum(
            "hqk,khd->qhd", weights, near_values, preferred_element_type=jnp.float32
        )
        return mixed_rows.reshape(block_rows, features)

    starts = jnp.arange(tok_rows // block_rows) * block_rows
    attended = lax.map(attend_block, starts).reshape(tok_rows, features)
    squares = jnp.sum(attended * attended, axis=1)
    total_sq = lax.psum(squares, "head")
    scale_rows = lax.rsqrt(total_sq / (features * lax.axis_size("head")) + 1e-06)
    normed_out = (attended * out_gain[None, :] * scale_rows[:, None]).astype(jnp.bfloat16)
    return (delta_out, normed_out)


def solution(mesh):
    placed = (
        P("seq", "head"),
        P("seq", "head"),
        P("seq", "head"),
        P("seq", "head"),
        P("seq", "head"),
        P("seq", "head"),
        P("head"),
    )
    return jax.shard_map(
        on_device,
        mesh=mesh,
        in_specs=placed,
        out_specs=(P("seq", "head"), P("seq", "head")),
        check_vma=False,
    )
```

```python
import math

import jax
import jax.numpy as jnp
from jax import lax
from jax.sharding import PartitionSpec as P

GROUP_TOKENS = 64
WINDOW = 2048


highest = lax.Precision.HIGHEST


def shifted(value, axis, by):
    size = lax.axis_size(axis)
    pairs = [(i, i + by) for i in range(size) if 0 <= i + by < size]
    return lax.ppermute(value, axis, pairs)


def unit_rows(entries):
    entries = entries.astype(jnp.float32)
    return entries * lax.rsqrt(jnp.sum(entries * entries, axis=-1, keepdims=True) + 1e-06)


def lower_inverse(below_part):
    length = below_part.shape[-1]
    identity = jnp.eye(length, dtype=jnp.float32)
    result = identity - below_part
    raised = below_part
    doubled = 2
    while doubled < length:
        raised = jnp.einsum("nij,njk->nik", raised, raised, precision=highest)
        result = jnp.einsum("nij,njk->nik", result, identity + raised, precision=highest)
        doubled = doubled * 2
    return result


def prepare(queries, key_rows, values, rate_rows):
    n_groups = queries.shape[0] // GROUP_TOKENS
    q_unit = unit_rows(queries).reshape(n_groups, GROUP_TOKENS, -1)
    k_unit = unit_rows(key_rows).reshape(n_groups, GROUP_TOKENS, -1)
    val_units = values.astype(jnp.float32).reshape(n_groups, GROUP_TOKENS, -1)
    rate_col = rate_rows.reshape(n_groups, GROUP_TOKENS, 1)
    key_inner = jnp.einsum("nik,njk->nij", k_unit, k_unit, precision=highest)
    positions = jnp.arange(GROUP_TOKENS)
    is_below = positions[:, None] > positions[None, :]
    on_or_below = positions[:, None] >= positions[None, :]
    below_part = jnp.where(is_below[None], rate_col * key_inner, 0.0)
    inverse = lower_inverse(below_part)
    writes = jnp.einsum("nij,njk->nik", inverse, rate_col * k_unit, precision=highest)
    updates = jnp.einsum("nij,njk->nik", inverse, rate_col * val_units, precision=highest)
    query_key = jnp.where(
        on_or_below[None], jnp.einsum("nik,njk->nij", q_unit, k_unit, precision=highest), 0.0
    )
    return (q_unit, k_unit, writes, updates, query_key)


def local_pair(k_unit, writes, updates):
    head_size = k_unit.shape[-1]
    identity = jnp.eye(head_size, dtype=jnp.float32)

    def stride(carry, inputs_now):
        transit, carried = carry
        k_block, w_block, u_block = inputs_now
        stepped = identity - jnp.dot(k_block.T, w_block, precision=highest)
        transit = jnp.dot(stepped, transit, precision=highest)
        carried = jnp.dot(stepped, carried, precision=highest) + jnp.dot(
            k_block.T, u_block, precision=highest
        )
        return ((transit, carried), None)

    start_pair = (identity, jnp.zeros((head_size, head_size), jnp.float32))
    (transit, carried), _ = lax.scan(stride, start_pair, (k_unit, writes, updates))
    return (transit, carried)


def advance(carried, inputs_now):
    q_block, k_block, w_block, u_block, cross_block = inputs_now
    corrected = u_block - jnp.dot(w_block, carried, precision=highest)
    result_now = jnp.dot(q_block, carried, precision=highest) + jnp.dot(
        cross_block, corrected, precision=highest
    )
    return (carried + jnp.dot(k_block.T, corrected, precision=highest), result_now)


def run_blocks(carried_in, q_unit, k_unit, writes, updates, query_key):
    _, results = lax.scan(advance, carried_in, (q_unit, k_unit, writes, updates, query_key))
    return results


def batched_dot(left, right):
    return jnp.einsum("hij,hjk->hik", left, right, precision=highest)


def on_device(q_delta, k_delta, v_delta, write_rate, q_attn, k_attn, out_gain):
    tok_rows, features = q_delta.shape
    heads_here = write_rate.shape[1]
    head_size = features // heads_here

    def by_head(entries):
        return entries.reshape(tok_rows, heads_here, head_size).transpose(1, 0, 2)

    q_unit, k_unit, writes, updates, query_key = jax.vmap(prepare)(
        by_head(q_delta), by_head(k_delta), by_head(v_delta), write_rate.T
    )
    transit, carried = jax.vmap(local_pair)(k_unit, writes, updates)
    position = lax.axis_index("seq")
    seq_size = lax.axis_size("seq")
    group = min(4, seq_size)
    rank = position % group

    def moved(value, by, sources):
        pairs = [(i, i + by) for i in sources if 0 <= i + by < seq_size]
        return lax.ppermute(value, "seq", pairs)

    identity = jnp.broadcast_to(jnp.eye(head_size, dtype=jnp.float32), transit.shape)
    before_transit = identity
    before_carried = jnp.zeros_like(carried)
    distance = 1
    while distance < group:
        inside = [i for i in range(seq_size) if i % group + distance < group]
        transit_prev = moved(transit, distance, inside)
        carried_prev = moved(carried, distance, inside)
        has_prev = rank >= distance
        before_carried = jnp.where(
            has_prev, batched_dot(before_transit, carried_prev) + before_carried, before_carried
        )
        before_transit = jnp.where(has_prev, batched_dot(before_transit, transit_prev), before_transit)
        carried_in = jnp.where(has_prev, batched_dot(transit, carried_prev) + carried, carried)
        transit = jnp.where(has_prev, batched_dot(transit, transit_prev), transit)
        carried = carried_in
        distance *= 2
    ends = [i for i in range(seq_size) if i % group == group - 1]
    end_transit, end_carried = transit, carried
    distance = group
    while distance < seq_size:
        final = 2 * distance >= seq_size
        carried_prev = moved(end_carried, distance, ends)
        has_prev = (rank == group - 1) & (position >= distance)
        carried_next = jnp.where(
            has_prev, batched_dot(end_transit, carried_prev) + end_carried, end_carried
        )
        if not final:
            transit_prev = moved(end_transit, distance, ends)
            end_transit = jnp.where(has_prev, batched_dot(end_transit, transit_prev), end_transit)
        end_carried = carried_next
        distance *= 2
    group_in = jnp.zeros_like(carried)
    for hop in range(1, group + 1):
        group_in = group_in + moved(end_carried, hop, ends)
    incoming = batched_dot(before_transit, group_in) + before_carried
    results = jax.vmap(run_blocks)(incoming, q_unit, k_unit, writes, updates, query_key)
    delta_out = (
        results.reshape(heads_here, tok_rows, head_size)
        .transpose(1, 0, 2)
        .reshape(tok_rows, features)
        .astype(jnp.bfloat16)
    )
    shard_reach = WINDOW // tok_rows

    def window_rows(own, lanes):
        lane_length = -(-shard_reach // lanes)
        pieces = []
        for lane in range(lanes):
            first = lane * lane_length + 1
            last = min(shard_reach, (lane + 1) * lane_length)
            piece = shifted(own, "seq", first)
            pieces.append(piece)
            for _ in range(first, last):
                piece = shifted(piece, "seq", 1)
                pieces.append(piece)
        return jnp.concatenate(pieces[::-1] + [own], axis=0)

    def bypass_rows(own):
        through = [i for i in range(seq_size) if i % group != group - 1]
        skipping = [i for i in range(seq_size) if i % group == group - 2]
        starts = rank == 0
        pieces = [own, shifted(own, "seq", 1)]
        for step in range(2, shard_reach + 1):
            near = moved(pieces[step - 1], 1, through)
            far = moved(pieces[step - 2], 2, skipping)
            pieces.append(jnp.where(starts, far, near))
        return jnp.concatenate(pieces[:0:-1] + [own], axis=0)

    rows_all = (bypass_rows(k_attn), window_rows(delta_out, 2))
    block_rows = min(512, tok_rows)
    first_row = lax.axis_index("seq") * tok_rows
    score_scale = 1.0 / math.sqrt(head_size)

    def attend_block(block_start):
        queries = q_attn.reshape(block_rows, heads_here, head_size)
        near_keys = rows_all[0].reshape(WINDOW + block_rows, heads_here, head_size)
        near_values = rows_all[1].reshape(WINDOW + block_rows, heads_here, head_size)
        scores = (
            jnp.einsum("qhd,khd->hqk", queries, near_keys, preferred_element_type=jnp.float32)
            * score_scale
        )
        q_index = jnp.arange(block_rows)[:, None]
        k_index = jnp.arange(WINDOW + block_rows)[None, :]
        allowed = (
            (k_index > q_index)
            & (k_index <= q_index + WINDOW)
            & (first_row + block_start + k_index >= WINDOW)
        )
        row_top = jnp.max(jnp.where(allowed[None], scores, -1e30), axis=2, keepdims=True)
        exps = jnp.exp(jnp.where(allowed[None], scores - row_top, -1e30))
        weights = (exps / jnp.sum(exps, axis=2, keepdims=True)).astype(jnp.bfloat16)
        mixed_rows = jnp.einsum(
            "hqk,khd->qhd", weights, near_values, preferred_element_type=jnp.float32
        )
        return mixed_rows.reshape(block_rows, features)

    starts = jnp.arange(tok_rows // block_rows) * block_rows
    attended = lax.map(attend_block, starts).reshape(tok_rows, features)
    squares = jnp.sum(attended * attended, axis=1)
    total_sq = lax.psum(squares, "head")
    scale_rows = lax.rsqrt(total_sq / (features * lax.axis_size("head")) + 1e-06)
    normed_out = (attended * out_gain[None, :] * scale_rows[:, None]).astype(jnp.bfloat16)
    return (delta_out, normed_out)


def solution(mesh):
    placed = (
        P("seq", "head"),
        P("seq", "head"),
        P("seq", "head"),
        P("seq", "head"),
        P("seq", "head"),
        P("seq", "head"),
        P("head"),
    )
    return jax.shard_map(
        on_device,
        mesh=mesh,
        in_specs=placed,
        out_specs=(P("seq", "head"), P("seq", "head")),
        check_vma=False,
    )
```

```python
import math

import jax
import jax.numpy as jnp
from jax import lax
from jax.sharding import PartitionSpec as P

GROUP_TOKENS = 64
WINDOW = 2048


highest = lax.Precision.HIGHEST


def shifted(value, axis, by):
    size = lax.axis_size(axis)
    pairs = [(i, i + by) for i in range(size) if 0 <= i + by < size]
    return lax.ppermute(value, axis, pairs)


def unit_rows(entries):
    entries = entries.astype(jnp.float32)
    return entries * lax.rsqrt(jnp.sum(entries * entries, axis=-1, keepdims=True) + 1e-06)


def lower_inverse(below_part):
    length = below_part.shape[-1]
    identity = jnp.eye(length, dtype=jnp.float32)
    result = identity - below_part
    raised = below_part
    doubled = 2
    while doubled < length:
        raised = jnp.einsum("nij,njk->nik", raised, raised, precision=highest)
        result = jnp.einsum("nij,njk->nik", result, identity + raised, precision=highest)
        doubled = doubled * 2
    return result


def prepare(queries, key_rows, values, rate_rows):
    n_groups = queries.shape[0] // GROUP_TOKENS
    q_unit = unit_rows(queries).reshape(n_groups, GROUP_TOKENS, -1)
    k_unit = unit_rows(key_rows).reshape(n_groups, GROUP_TOKENS, -1)
    val_units = values.astype(jnp.float32).reshape(n_groups, GROUP_TOKENS, -1)
    rate_col = rate_rows.reshape(n_groups, GROUP_TOKENS, 1)
    key_inner = jnp.einsum("nik,njk->nij", k_unit, k_unit, precision=highest)
    positions = jnp.arange(GROUP_TOKENS)
    is_below = positions[:, None] > positions[None, :]
    on_or_below = positions[:, None] >= positions[None, :]
    below_part = jnp.where(is_below[None], rate_col * key_inner, 0.0)
    inverse = lower_inverse(below_part)
    writes = jnp.einsum("nij,njk->nik", inverse, rate_col * k_unit, precision=highest)
    updates = jnp.einsum("nij,njk->nik", inverse, rate_col * val_units, precision=highest)
    query_key = jnp.where(
        on_or_below[None], jnp.einsum("nik,njk->nij", q_unit, k_unit, precision=highest), 0.0
    )
    return (q_unit, k_unit, writes, updates, query_key)


def local_pair(k_unit, writes, updates):
    head_size = k_unit.shape[-1]
    identity = jnp.eye(head_size, dtype=jnp.float32)

    def stride(carry, inputs_now):
        transit, carried = carry
        k_block, w_block, u_block = inputs_now
        stepped = identity - jnp.dot(k_block.T, w_block, precision=highest)
        transit = jnp.dot(stepped, transit, precision=highest)
        carried = jnp.dot(stepped, carried, precision=highest) + jnp.dot(
            k_block.T, u_block, precision=highest
        )
        return ((transit, carried), None)

    start_pair = (identity, jnp.zeros((head_size, head_size), jnp.float32))
    (transit, carried), _ = lax.scan(stride, start_pair, (k_unit, writes, updates))
    return (transit, carried)


def advance(carried, inputs_now):
    q_block, k_block, w_block, u_block, cross_block = inputs_now
    corrected = u_block - jnp.dot(w_block, carried, precision=highest)
    result_now = jnp.dot(q_block, carried, precision=highest) + jnp.dot(
        cross_block, corrected, precision=highest
    )
    return (carried + jnp.dot(k_block.T, corrected, precision=highest), result_now)


def run_blocks(carried_in, q_unit, k_unit, writes, updates, query_key):
    _, results = lax.scan(advance, carried_in, (q_unit, k_unit, writes, updates, query_key))
    return results


def batched_dot(left, right):
    return jnp.einsum("hij,hjk->hik", left, right, precision=highest)


def on_device(q_delta, k_delta, v_delta, write_rate, q_attn, k_attn, out_gain):
    tok_rows, features = q_delta.shape
    heads_here = write_rate.shape[1]
    head_size = features // heads_here

    def by_head(entries):
        return entries.reshape(tok_rows, heads_here, head_size).transpose(1, 0, 2)

    q_unit, k_unit, writes, updates, query_key = jax.vmap(prepare)(
        by_head(q_delta), by_head(k_delta), by_head(v_delta), write_rate.T
    )
    transit, carried = jax.vmap(local_pair)(k_unit, writes, updates)
    position = lax.axis_index("seq")
    seq_size = lax.axis_size("seq")
    group = min(4, seq_size)
    rank = position % group

    def moved(value, by, sources):
        pairs = [(i, i + by) for i in sources if 0 <= i + by < seq_size]
        return lax.ppermute(value, "seq", pairs)

    identity = jnp.broadcast_to(jnp.eye(head_size, dtype=jnp.float32), transit.shape)
    before_transit = identity
    before_carried = jnp.zeros_like(carried)
    distance = 1
    while distance < group:
        inside = [i for i in range(seq_size) if i % group + distance < group]
        transit_prev = moved(transit, distance, inside)
        carried_prev = moved(carried, distance, inside)
        has_prev = rank >= distance
        before_carried = jnp.where(
            has_prev, batched_dot(before_transit, carried_prev) + before_carried, before_carried
        )
        before_transit = jnp.where(has_prev, batched_dot(before_transit, transit_prev), before_transit)
        carried_in = jnp.where(has_prev, batched_dot(transit, carried_prev) + carried, carried)
        transit = jnp.where(has_prev, batched_dot(transit, transit_prev), transit)
        carried = carried_in
        distance *= 2
    ends = [i for i in range(seq_size) if i % group == group - 1]
    end_transit, end_carried = transit, carried
    distance = group
    while distance < seq_size:
        final = 2 * distance >= seq_size
        carried_prev = moved(end_carried, distance, ends)
        has_prev = (rank == group - 1) & (position >= distance)
        carried_next = jnp.where(
            has_prev, batched_dot(end_transit, carried_prev) + end_carried, end_carried
        )
        if not final:
            transit_prev = moved(end_transit, distance, ends)
            end_transit = jnp.where(has_prev, batched_dot(end_transit, transit_prev), end_transit)
        end_carried = carried_next
        distance *= 2
    group_in = jnp.zeros_like(carried)
    for hop in range(1, group + 1):
        group_in = group_in + moved(end_carried, hop, ends)
    incoming = batched_dot(before_transit, group_in) + before_carried
    results = jax.vmap(run_blocks)(incoming, q_unit, k_unit, writes, updates, query_key)
    delta_out = (
        results.reshape(heads_here, tok_rows, head_size)
        .transpose(1, 0, 2)
        .reshape(tok_rows, features)
        .astype(jnp.bfloat16)
    )
    shard_reach = WINDOW // tok_rows

    def window_rows(own, lanes):
        lane_length = -(-shard_reach // lanes)
        pieces = []
        for lane in range(lanes):
            first = lane * lane_length + 1
            last = min(shard_reach, (lane + 1) * lane_length)
            piece = shifted(own, "seq", first)
            pieces.append(piece)
            for _ in range(first, last):
                piece = shifted(piece, "seq", 1)
                pieces.append(piece)
        return jnp.concatenate(pieces[::-1] + [own], axis=0)

    rows_all = (window_rows(k_attn, 1), window_rows(delta_out, 2))
    block_rows = min(512, tok_rows)
    first_row = lax.axis_index("seq") * tok_rows
    score_scale = 1.0 / math.sqrt(head_size)

    def attend_block(block_start):
        queries = q_attn.reshape(block_rows, heads_here, head_size)
        near_keys = rows_all[0].reshape(WINDOW + block_rows, heads_here, head_size)
        near_values = rows_all[1].reshape(WINDOW + block_rows, heads_here, head_size)
        scores = (
            jnp.einsum("qhd,khd->hqk", queries, near_keys, preferred_element_type=jnp.float32)
            * score_scale
        )
        q_index = jnp.arange(block_rows)[:, None]
        k_index = jnp.arange(WINDOW + block_rows)[None, :]
        allowed = (
            (k_index > q_index)
            & (k_index <= q_index + WINDOW)
            & (first_row + block_start + k_index >= WINDOW)
        )
        row_top = jnp.max(jnp.where(allowed[None], scores, -1e30), axis=2, keepdims=True)
        exps = jnp.exp(jnp.where(allowed[None], scores - row_top, -1e30))
        weights = (exps / jnp.sum(exps, axis=2, keepdims=True)).astype(jnp.bfloat16)
        mixed_rows = jnp.einsum(
            "hqk,khd->qhd", weights, near_values, preferred_element_type=jnp.float32
        )
        return mixed_rows.reshape(block_rows, features)

    starts = jnp.arange(tok_rows // block_rows) * block_rows
    attended = lax.map(attend_block, starts).reshape(tok_rows, features)
    squares = jnp.sum(attended * attended, axis=1)
    total_sq = jnp.sum(lax.all_gather(squares, "head"), axis=0)
    scale_rows = lax.rsqrt(total_sq / (features * lax.axis_size("head")) + 1e-06)
    normed_out = (attended * out_gain[None, :] * scale_rows[:, None]).astype(jnp.bfloat16)
    return (delta_out, normed_out)


def solution(mesh):
    placed = (
        P("seq", "head"),
        P("seq", "head"),
        P("seq", "head"),
        P("seq", "head"),
        P("seq", "head"),
        P("seq", "head"),
        P("head"),
    )
    return jax.shard_map(
        on_device,
        mesh=mesh,
        in_specs=placed,
        out_specs=(P("seq", "head"), P("seq", "head")),
        check_vma=False,
    )
```

```python
import math

import jax
import jax.numpy as jnp
from jax import lax
from jax.sharding import PartitionSpec as P

GROUP_TOKENS = 64
WINDOW = 2048


highest = lax.Precision.HIGHEST


def shifted(value, axis, by):
    size = lax.axis_size(axis)
    pairs = [(i, i + by) for i in range(size) if 0 <= i + by < size]
    return lax.ppermute(value, axis, pairs)


def unit_rows(entries):
    entries = entries.astype(jnp.float32)
    return entries * lax.rsqrt(jnp.sum(entries * entries, axis=-1, keepdims=True) + 1e-06)


def lower_inverse(below_part):
    length = below_part.shape[-1]
    identity = jnp.eye(length, dtype=jnp.float32)
    result = identity - below_part
    raised = below_part
    doubled = 2
    while doubled < length:
        raised = jnp.einsum("nij,njk->nik", raised, raised, precision=highest)
        result = jnp.einsum("nij,njk->nik", result, identity + raised, precision=highest)
        doubled = doubled * 2
    return result


def prepare(queries, key_rows, values, rate_rows):
    n_groups = queries.shape[0] // GROUP_TOKENS
    q_unit = unit_rows(queries).reshape(n_groups, GROUP_TOKENS, -1)
    k_unit = unit_rows(key_rows).reshape(n_groups, GROUP_TOKENS, -1)
    val_units = values.astype(jnp.float32).reshape(n_groups, GROUP_TOKENS, -1)
    rate_col = rate_rows.reshape(n_groups, GROUP_TOKENS, 1)
    key_inner = jnp.einsum("nik,njk->nij", k_unit, k_unit, precision=highest)
    positions = jnp.arange(GROUP_TOKENS)
    is_below = positions[:, None] > positions[None, :]
    on_or_below = positions[:, None] >= positions[None, :]
    below_part = jnp.where(is_below[None], rate_col * key_inner, 0.0)
    inverse = lower_inverse(below_part)
    writes = jnp.einsum("nij,njk->nik", inverse, rate_col * k_unit, precision=highest)
    updates = jnp.einsum("nij,njk->nik", inverse, rate_col * val_units, precision=highest)
    query_key = jnp.where(
        on_or_below[None], jnp.einsum("nik,njk->nij", q_unit, k_unit, precision=highest), 0.0
    )
    return (q_unit, k_unit, writes, updates, query_key)


def local_pair(k_unit, writes, updates):
    head_size = k_unit.shape[-1]
    identity = jnp.eye(head_size, dtype=jnp.float32)

    def stride(carry, inputs_now):
        transit, carried = carry
        k_block, w_block, u_block = inputs_now
        stepped = identity - jnp.dot(k_block.T, w_block, precision=highest)
        transit = jnp.dot(stepped, transit, precision=highest)
        carried = jnp.dot(stepped, carried, precision=highest) + jnp.dot(
            k_block.T, u_block, precision=highest
        )
        return ((transit, carried), None)

    start_pair = (identity, jnp.zeros((head_size, head_size), jnp.float32))
    (transit, carried), _ = lax.scan(stride, start_pair, (k_unit, writes, updates))
    return (transit, carried)


def local_affine(q_unit, k_unit, writes, updates, query_key):
    n_blocks, _, head_size = k_unit.shape
    identity = jnp.eye(head_size, dtype=jnp.float32)
    key_cols = jnp.swapaxes(k_unit, -1, -2)
    stepped = identity - jnp.einsum("nij,njk->nik", key_cols, writes, precision=highest)
    written = jnp.einsum("nij,njk->nik", key_cols, updates, precision=highest)
    transit_list = [identity]
    carried_list = [jnp.zeros_like(identity)]
    for block in range(n_blocks):
        transit_list.append(jnp.dot(stepped[block], transit_list[-1], precision=highest))
        carried_list.append(
            jnp.dot(stepped[block], carried_list[-1], precision=highest) + written[block]
        )
    transit_before = jnp.stack(transit_list[:-1])
    carried_before = jnp.stack(carried_list[:-1])
    reading = q_unit - jnp.einsum("nij,njk->nik", query_key, writes, precision=highest)
    slope = jnp.einsum("nij,njk->nik", reading, transit_before, precision=highest)
    offset = jnp.einsum("nij,njk->nik", reading, carried_before, precision=highest) + jnp.einsum(
        "nij,njk->nik", query_key, updates, precision=highest
    )
    rows = n_blocks * k_unit.shape[1]
    return (
        transit_list[-1],
        carried_list[-1],
        slope.reshape(rows, head_size),
        offset.reshape(rows, head_size),
    )


def advance(carried, inputs_now):
    q_block, k_block, w_block, u_block, cross_block = inputs_now
    corrected = u_block - jnp.dot(w_block, carried, precision=highest)
    result_now = jnp.dot(q_block, carried, precision=highest) + jnp.dot(
        cross_block, corrected, precision=highest
    )
    return (carried + jnp.dot(k_block.T, corrected, precision=highest), result_now)


def run_blocks(carried_in, q_unit, k_unit, writes, updates, query_key):
    _, results = lax.scan(advance, carried_in, (q_unit, k_unit, writes, updates, query_key))
    return results


def batched_dot(left, right):
    return jnp.einsum("hij,hjk->hik", left, right, precision=highest)


def on_device(q_delta, k_delta, v_delta, write_rate, q_attn, k_attn, out_gain):
    tok_rows, features = q_delta.shape
    heads_here = write_rate.shape[1]
    head_size = features // heads_here

    def by_head(entries):
        return entries.reshape(tok_rows, heads_here, head_size).transpose(1, 0, 2)

    q_unit, k_unit, writes, updates, query_key = jax.vmap(prepare)(
        by_head(q_delta), by_head(k_delta), by_head(v_delta), write_rate.T
    )
    transit, carried, slope, offset = jax.vmap(local_affine)(
        q_unit, k_unit, writes, updates, query_key
    )
    position = lax.axis_index("seq")
    seq_size = lax.axis_size("seq")
    group = min(4, seq_size)
    rank = position % group

    def moved(value, by, sources):
        pairs = [(i, i + by) for i in sources if 0 <= i + by < seq_size]
        return lax.ppermute(value, "seq", pairs)

    identity = jnp.broadcast_to(jnp.eye(head_size, dtype=jnp.float32), transit.shape)
    before_transit = identity
    before_carried = jnp.zeros_like(carried)
    distance = 1
    while distance < group:
        inside = [i for i in range(seq_size) if i % group + distance < group]
        transit_prev = moved(transit, distance, inside)
        carried_prev = moved(carried, distance, inside)
        has_prev = rank >= distance
        before_carried = jnp.where(
            has_prev, batched_dot(before_transit, carried_prev) + before_carried, before_carried
        )
        before_transit = jnp.where(has_prev, batched_dot(before_transit, transit_prev), before_transit)
        carried_in = jnp.where(has_prev, batched_dot(transit, carried_prev) + carried, carried)
        transit = jnp.where(has_prev, batched_dot(transit, transit_prev), transit)
        carried = carried_in
        distance *= 2
    ends = [i for i in range(seq_size) if i % group == group - 1]
    end_transit, end_carried = transit, carried
    distance = group
    while distance < seq_size:
        final = 2 * distance >= seq_size
        carried_prev = moved(end_carried, distance, ends)
        has_prev = (rank == group - 1) & (position >= distance)
        carried_next = jnp.where(
            has_prev, batched_dot(end_transit, carried_prev) + end_carried, end_carried
        )
        if not final:
            transit_prev = moved(end_transit, distance, ends)
            end_transit = jnp.where(has_prev, batched_dot(end_transit, transit_prev), end_transit)
        end_carried = carried_next
        distance *= 2
    group_in = jnp.zeros_like(carried)
    for hop in range(1, group + 1):
        group_in = group_in + moved(end_carried, hop, ends)
    offset = offset + batched_dot(slope, before_carried)
    slope = batched_dot(slope, before_transit)
    results = batched_dot(slope, group_in) + offset
    delta_out = (
        results.reshape(heads_here, tok_rows, head_size)
        .transpose(1, 0, 2)
        .reshape(tok_rows, features)
        .astype(jnp.bfloat16)
    )
    shard_reach = WINDOW // tok_rows

    def window_rows(own, lanes):
        lane_length = -(-shard_reach // lanes)
        pieces = []
        for lane in range(lanes):
            first = lane * lane_length + 1
            last = min(shard_reach, (lane + 1) * lane_length)
            piece = shifted(own, "seq", first)
            pieces.append(piece)
            for _ in range(first, last):
                piece = shifted(piece, "seq", 1)
                pieces.append(piece)
        return jnp.concatenate(pieces[::-1] + [own], axis=0)

    rows_all = (window_rows(k_attn, 1), window_rows(delta_out, 2))
    block_rows = min(512, tok_rows)
    first_row = lax.axis_index("seq") * tok_rows
    score_scale = 1.0 / math.sqrt(head_size)

    def attend_block(block_start):
        queries = q_attn.reshape(block_rows, heads_here, head_size)
        near_keys = rows_all[0].reshape(WINDOW + block_rows, heads_here, head_size)
        near_values = rows_all[1].reshape(WINDOW + block_rows, heads_here, head_size)
        scores = (
            jnp.einsum("qhd,khd->hqk", queries, near_keys, preferred_element_type=jnp.float32)
            * score_scale
        )
        q_index = jnp.arange(block_rows)[:, None]
        k_index = jnp.arange(WINDOW + block_rows)[None, :]
        allowed = (
            (k_index > q_index)
            & (k_index <= q_index + WINDOW)
            & (first_row + block_start + k_index >= WINDOW)
        )
        row_top = jnp.max(jnp.where(allowed[None], scores, -1e30), axis=2, keepdims=True)
        exps = jnp.exp(jnp.where(allowed[None], scores - row_top, -1e30))
        weights = (exps / jnp.sum(exps, axis=2, keepdims=True)).astype(jnp.bfloat16)
        mixed_rows = jnp.einsum(
            "hqk,khd->qhd", weights, near_values, preferred_element_type=jnp.float32
        )
        return mixed_rows.reshape(block_rows, features)

    starts = jnp.arange(tok_rows // block_rows) * block_rows
    attended = lax.map(attend_block, starts).reshape(tok_rows, features)
    squares = jnp.sum(attended * attended, axis=1)
    total_sq = jnp.sum(lax.all_gather(squares, "head"), axis=0)
    scale_rows = lax.rsqrt(total_sq / (features * lax.axis_size("head")) + 1e-06)
    normed_out = (attended * out_gain[None, :] * scale_rows[:, None]).astype(jnp.bfloat16)
    return (delta_out, normed_out)


def solution(mesh):
    placed = (
        P("seq", "head"),
        P("seq", "head"),
        P("seq", "head"),
        P("seq", "head"),
        P("seq", "head"),
        P("seq", "head"),
        P("head"),
    )
    return jax.shard_map(
        on_device,
        mesh=mesh,
        in_specs=placed,
        out_specs=(P("seq", "head"), P("seq", "head")),
        check_vma=False,
    )
```
